512 devices in a mesh: sec: 4 (over x), tile: 32 (over z, core), lev: 4 (over y).
Axes of the slice: x: 4, y: 4, z: 16, core: 2. Of those that a mesh axis runs over, the one named last changes fastest.
Arguments:
- ocean_conc: float32 [8, 4096, 512], P('lev', ('sec', 'tile')), may hold values from 0.1 to 2.9
- flow_lo: bfloat16 [4096, 512], P(('sec', 'tile')), as said below
- flow_hi: bfloat16 [4096, 512], P(('sec', 'tile')), as said below
- flow_y: bfloat16 [4096, 512], P(('sec', 'tile')), as said below
- open_lo: int32 [4096, 512], P(('sec', 'tile')), may hold values from 0 to 1, as said below
- open_hi: int32 [4096, 512], P(('sec', 'tile')), may hold values from 0 to 1
- open_y: int32 [4096, 512], P(('sec', 'tile')), may hold values from 0 to 1, as said below
- settle_rate: float32 [8], P('lev'), may hold values from 0.01 to 0.1
- critical_stress: float32 [8], P('lev'), may hold values from 0.05 to 0.5
- erosion_rate: float32 [8], P('lev'), may hold values from 0.002 to 0.02
- wave_energy: bfloat16 [768, 65536], P('lev', ('sec', 'tile')), may hold values from 0 to 2
- band_angle: float32 [768], P('lev'), may hold values from -3.140625 to 3.140625
- band_speed: float32 [768], P('lev'), may hold values from 0.2 to 0.3
- band_growth: float32 [768], P('lev'), may hold values from 0.05 to 0.5
- band_orbital: float32 [768], P('lev'), may hold values from 0.01 to 0.1
- neighbors: int32 [4, 65536], P(None, ('sec', 'tile')), may hold values from 0 to 65535, as said below
- facing_angle: float32 [4, 65536], P(None, ('sec', 'tile')), may hold values from -3.140625 to 3.140625
- live_nodes: int32 [65536], P(('sec', 'tile')), may hold values 0 or 1
- remap_owner: int32 [8192, 1], P(('sec', 'tile')), may hold values from 0 to 127; in each aligned block of 64 rows (0 to 63, 64 to 127, ...) at most 2 rows name the same one
- remap_slot: int32 [8192], P(('sec', 'tile')), may hold values from 0 to 7
- remap_cell: int32 [8192], P(('sec', 'tile')), may hold values from 0 to 255
- remap_weight: bfloat16 [8192, 64, 64], P(('sec', 'tile')), may hold values from -0.25 to 0.25
Outputs:
- sediment_out: float32 [8, 4096, 512], P('lev', ('sec', 'tile'))
- waves_out: bfloat16 [768, 65536], P('lev', ('sec', 'tile'))
The draws below stay inside these ranges and needn't reach their ends.
Inputs may be any that keep to these rules, and one draw needn't show every extreme that they name: open_hi of row r equals open_lo of row r + 1; the lower face of the first row and the upper face of the last row are closed. `open_y`: the face after the last column is closed. flow_lo is zero where open_lo is 0, of magnitude at most 0.150390625; flow_hi of row r equals flow_lo of row r + 1. `flow_hi`: zero where open_hi is 0, of magnitude at most 0.150390625. `flow_y`: zero where open_y is 0, of magnitude at most 0.150390625. `neighbors`: each neighbour's index differs from its node's index by at most 128. `remap_owner`: among the 64 entries of one device at most 2 name the same owner.
All inputs are finite; a program needn't handle non-finite values. No bound on the sum of `live_nodes` on one device may be relied on, other than what follows from the above.
Results may differ from the reference program's by a relative error of at most 0.001.
Values sent between devices are 32-bit elements; how exact they have to be, the bound alone decides.
No kernel may reach another device: no remote copies, remote signals or barrier semaphores. Data moves between devices by JAX's collectives and lax.ppermute only.
A program may use at most 64 MiB of HBM per device.

```python
import math
import jax
import jax.numpy as jnp
import numpy as np
from jax import lax

OY = 512
OSTEPS = 4
BANDS = 768
WSTEPS = 4
NBRS = 4
ENT = 64
PEERS = 128
CLASSES = 8
OX = 4096
OB_DEV = 256
WNODES = 65536
WB_DEV = 8
CAP = 2


def open_faces_x(key):
    interior = (jax.random.randint(jax.random.fold_in(key, 101), (OX - 1, OY), 0, 8) < 7).astype(jnp.int32)
    closed = jnp.zeros((1, OY), jnp.int32)
    return jnp.concatenate([closed, interior, closed], axis=0)


def open_faces_y(key):
    interior = (jax.random.randint(jax.random.fold_in(key, 102), (OX, OY - 1), 0, 8) < 7).astype(jnp.int32)
    return jnp.concatenate([interior, jnp.zeros((OX, 1), jnp.int32)], axis=1)


def face_speed(key, extent):
    return jax.random.uniform(key, extent, jnp.float32, -0.15, 0.15)


def current_speed_x(key, extent):
    column_sign = jnp.where(jax.random.uniform(jax.random.fold_in(key, 3), (1, extent[1]), jnp.float32) < 0.5, -1.0, 1.0)
    magnitude = jax.random.uniform(jax.random.fold_in(key, 1), extent, jnp.float32, 0.65, 1.0)
    return 0.15 * magnitude * column_sign


def faces_x_flow(key):
    return current_speed_x(jax.random.fold_in(key, 103), (OX + 1, OY)) * open_faces_x(key).astype(jnp.float32)


def draw_flow_lo(key, part):
    return faces_x_flow(key)[:-1].astype(jnp.bfloat16)


def draw_flow_hi(key, part):
    return faces_x_flow(key)[1:].astype(jnp.bfloat16)


def draw_flow_y(key, part):
    speed_field = face_speed(jax.random.fold_in(key, 104), (OX, OY)) * open_faces_y(key).astype(jnp.float32)
    return speed_field.astype(jnp.bfloat16)


def draw_open_lo(key, part):
    return open_faces_x(key)[:-1]


def draw_open_hi(key, part):
    return open_faces_x(key)[1:]


def draw_open_y(key, part):
    return open_faces_y(key)


def draw_neighbors(key, part):
    nodes = jnp.arange(WNODES, dtype=jnp.int32)
    far_reach = jax.random.randint(jax.random.fold_in(key, 105), (2, WNODES), 96, 129)
    far_reach = jnp.where((nodes % 64 == 0)[None, :], 128, far_reach)
    near_reach = jax.random.randint(jax.random.fold_in(key, 106), (2, WNODES), -128, 129)
    offsets = jnp.concatenate([-far_reach[0:1], far_reach[1:2], near_reach], axis=0)
    return jnp.clip(nodes[None, :] + offsets, 0, WNODES - 1).astype(jnp.int32)


def place_ends(values, rng, least, top_value):
    longest = values.shape.index(max(values.shape))
    spots = []
    for shift in (0, 1):
        where = [jax.random.randint(jax.random.fold_in(rng, axis), (), 0, length) for axis, length in enumerate(values.shape)]
        where[longest] = (where[longest] + shift) % values.shape[longest]
        spots.append(tuple(where))
    return values.at[spots[0]].set(least).at[spots[1]].set(top_value)


def block_levels(own_key, dims, split, least, high):
    loudness, own = 1.0, jax.random.fold_in(own_key, 6)
    for axis_at, shards_of in split:
        heights = jnp.exp(jax.random.uniform(jax.random.fold_in(own, axis_at), (shards_of,), jnp.float32, least / len(split), high / len(split)))
        loudness = loudness * jnp.repeat(heights, dims[axis_at] // shards_of).reshape([-1 if axis == axis_at else 1 for axis in range(len(dims))])
    return loudness


def shared_out(rng, own, number, rows, number_of, top, reach, lean):
    ranking = jax.random.permutation(rng, number_of)
    heavy_load, common = portions_of(number_of, rows * top, reach, lean, True), portions_of(number_of, rows * top, reach, lean, False)
    places = jnp.arange(number_of)

    def named(lengths, offset_by):
        used = int((lengths > 0).sum())
        fixed = max(1, used // 4)
        moved = fixed + (places - fixed + offset_by * (used - fixed)) % max(1, number_of - fixed)
        return jnp.zeros((number_of,), jnp.int32).at[ranking[jnp.where(places < fixed, places, moved)]].set(jnp.asarray(lengths, jnp.int32))

    lengths = jnp.where(number % 4 == 0, named(heavy_load, number // 4), named(common, number - number // 4 - 1))
    mixed = jax.random.permutation(jax.random.fold_in(own, 3), number_of)
    donor, sink = mixed[0:number_of // 2 * 2:2], mixed[1:number_of // 2 * 2:2]
    slack = jnp.minimum(lengths[donor] - 1, reach - lengths[sink]) // 2
    slack = jnp.where((donor == ranking[0]) | (sink == ranking[0]) | (lengths[sink] == 0), 0, jnp.maximum(slack, 0))
    moved = jax.random.randint(jax.random.fold_in(own, 4), (number_of // 2,), 0, 1 << 20) % (slack + 1)
    lengths = lengths.at[donor].add(-moved).at[sink].add(moved)
    members = jnp.searchsorted(jnp.cumsum(lengths), jnp.arange(rows * top), side="right").astype(jnp.int32)
    listing = members.reshape(top, rows).T
    listing = listing[jax.random.permutation(jax.random.fold_in(own, 1), rows)]
    offset_by = jax.random.randint(jax.random.fold_in(own, 2), (rows, 1), 0, top)
    return jnp.take_along_axis(listing, (jnp.arange(top)[None, :] + offset_by) % top, axis=1)


def portions_of(amount, total, most, lean, full):
    portions = [(1 << 20) // math.isqrt(standing ** lean) + 1 for standing in range(1, amount + 1)]
    largest = most if full else min(most, max(-(-total // amount), total * portions[0] // sum(portions)))
    least = 1 if total - largest >= amount - 1 else 0
    given, spare = [largest] + [least] * (amount - 1), total - largest - least * (amount - 1)
    while spare > 0:
        candidates = [i for i in range(1, amount) if given[i] < largest] or [i for i in range(1, amount) if given[i] < most]
        pool, left = sum([portions[i] for i in candidates]), spare
        for i in candidates:
            extra = min(most - given[i], max(1, left * portions[i] // pool), spare)
            given[i] = given[i] + extra
            spare = spare - extra
    return np.array(given)


def scatter_about(key, dims, scale, limit, split=(), kind=jnp.bfloat16):
    result = scale * jax.random.normal(key, dims, jnp.float32)
    if split:
        result = result * block_levels(key, dims, split, -0.22, 0.18)
    return jnp.clip(result, -limit, limit).astype(kind)


def setup_inputs(seed: int = 0) -> dict:
    arg_keys = jax.random.split(jax.random.key(seed), 23)
    ocean_conc = jnp.clip(0.1 + 2.8000001 * jax.random.uniform(arg_keys[0], (CLASSES, OX, OY), jnp.float32) ** block_levels(arg_keys[0], (CLASSES, OX, OY), ((0, 4), (1, 128)), -0.2, 0.2), 0.1, 2.9)
    flow_lo = draw_flow_lo(jax.random.fold_in(arg_keys[22], 71), 0)
    flow_hi = draw_flow_hi(jax.random.fold_in(arg_keys[22], 71), 0)
    flow_y = draw_flow_y(jax.random.fold_in(arg_keys[22], 71), 0)
    open_lo = draw_open_lo(jax.random.fold_in(arg_keys[22], 71), 0)
    open_hi = draw_open_hi(jax.random.fold_in(arg_keys[22], 71), 0)
    open_y = draw_open_y(jax.random.fold_in(arg_keys[22], 71), 0)
    settle_rate = jnp.clip(jnp.exp(math.log(0.1) - 2.3025851 * jax.random.uniform(arg_keys[7], (CLASSES,), jnp.float32) ** block_levels(arg_keys[7], (CLASSES,), ((0, 4),), -0.2, 0.2)), 0.01, 0.1)
    critical_stress = jnp.clip(jnp.exp(math.log(0.5) - 2.3025851 * jax.random.uniform(arg_keys[8], (CLASSES,), jnp.float32) ** block_levels(arg_keys[8], (CLASSES,), ((0, 4),), -0.2, 0.2)), 0.05, 0.5)
    erosion_rate = jnp.clip(jnp.exp(math.log(0.02) - 2.30258502 * jax.random.uniform(arg_keys[9], (CLASSES,), jnp.float32) ** block_levels(arg_keys[9], (CLASSES,), ((0, 4),), -0.2, 0.2)), 0.002, 0.02)
    wave_energy = jnp.clip(2.0 * jax.random.uniform(arg_keys[10], (BANDS, WNODES), jnp.float32) ** block_levels(arg_keys[10], (BANDS, WNODES), ((0, 4), (1, 128)), -0.2, 0.2), 0.0, 2.0).astype(jnp.bfloat16)
    band_angle = jnp.clip(jax.random.uniform(arg_keys[11], (BANDS,), jnp.float32, -3.140625, 3.140625), -3.140625, 3.140625)
    band_speed = jnp.clip(0.2 + 0.10000001 * jax.random.uniform(arg_keys[12], (BANDS,), jnp.float32) ** block_levels(arg_keys[12], (BANDS,), ((0, 4),), -0.2, 0.2), 0.2, 0.3)
    band_growth = jnp.clip(jnp.exp(math.log(0.5) - 2.3025851 * jax.random.uniform(arg_keys[13], (BANDS,), jnp.float32) ** block_levels(arg_keys[13], (BANDS,), ((0, 4),), -0.2, 0.2)), 0.05, 0.5)
    band_orbital = jnp.clip(jnp.exp(math.log(0.1) - 2.3025851 * jax.random.uniform(arg_keys[14], (BANDS,), jnp.float32) ** block_levels(arg_keys[14], (BANDS,), ((0, 4),), -0.2, 0.2)), 0.01, 0.1)
    neighbors = draw_neighbors(jax.random.fold_in(arg_keys[22], 71), 0)
    facing_angle = jnp.clip(jax.random.uniform(arg_keys[16], (NBRS, WNODES), jnp.float32, -3.140625, 3.140625), -3.140625, 3.140625)
    live_nodes = place_ends((jax.random.randint(arg_keys[17], (WNODES,), 0, 8) < 7).astype(jnp.int32), jax.random.fold_in(arg_keys[17], 1), 0, 1)
    remap_owner_keys = jax.random.split(jax.random.fold_in(arg_keys[18], 1), (PEERS * ENT) // ENT)
    remap_owner_turns = jax.random.permutation(jax.random.fold_in(arg_keys[18], 3), (PEERS * ENT) // ENT)
    remap_owner = jax.vmap(lambda own, number: shared_out(jax.random.fold_in(arg_keys[18], 2), own, number, ENT, PEERS, 1, CAP, 2))(remap_owner_keys, remap_owner_turns).reshape((PEERS * ENT, 1))
    remap_slot = place_ends(jax.random.randint(arg_keys[19], (PEERS * ENT,), 0, WB_DEV), jax.random.fold_in(arg_keys[19], 1), 0, WB_DEV - 1).astype(jnp.int32)
    remap_cell = place_ends(jax.random.randint(arg_keys[20], (PEERS * ENT,), 0, OB_DEV), jax.random.fold_in(arg_keys[20], 1), 0, OB_DEV - 1).astype(jnp.int32)
    remap_weight = scatter_about(arg_keys[21], (PEERS * ENT, 64, 64), (64 * ENT // WB_DEV) ** -0.5, 0.25, ((0, 128),))
    return {"ocean_conc": ocean_conc, "flow_lo": flow_lo, "flow_hi": flow_hi, "flow_y": flow_y, "open_lo": open_lo, "open_hi": open_hi, "open_y": open_y, "settle_rate": settle_rate, "critical_stress": critical_stress, "erosion_rate": erosion_rate, "wave_energy": wave_energy, "band_angle": band_angle, "band_speed": band_speed, "band_growth": band_growth, "band_orbital": band_orbital, "neighbors": neighbors, "facing_angle": facing_angle, "live_nodes": live_nodes, "remap_owner": remap_owner, "remap_slot": remap_slot, "remap_cell": remap_cell, "remap_weight": remap_weight}


KAPPA = 0.07
FORCE_SCALE = 5.0
DRAG = 50.0
TAU_CURRENT = 20.0
TAU_WAVES = 10.0
HIGHEST = lax.Precision.HIGHEST

def coupling_fields(flow_lo, flow_hi, flow_y):
    eastward = 0.5 * (flow_lo.astype(jnp.float32) + flow_hi.astype(jnp.float32))
    across = flow_y.astype(jnp.float32)
    earlier = jnp.pad(across, ((0, 0), (1, 0)))[:, :-1]
    northward = 0.5 * (across + earlier)
    current_speed = jnp.sqrt(eastward * eastward + northward * northward)
    forcing = jnp.stack([FORCE_SCALE * eastward, FORCE_SCALE * northward, DRAG * current_speed * eastward, DRAG * current_speed * northward])
    return (forcing, eastward * eastward + northward * northward)

def band_rates(wave_forcing, band_dir, band_pace, growth, facing):
    cosines = jnp.cos(band_dir)[:, None]
    sine_terms = jnp.sin(band_dir)[:, None]
    drift_term = cosines * wave_forcing[0][None, :] + sine_terms * wave_forcing[1][None, :]
    push_term = jnp.maximum(cosines * wave_forcing[2][None, :] + sine_terms * wave_forcing[3][None, :], 0.0)
    base_rate = 0.5 * band_pace[:, None] * (1.0 + 0.5 * jnp.tanh(drift_term))
    inflow = base_rate[None] * jnp.maximum(-jnp.cos(band_dir[None, :, None] - facing[:, None, :]), 0.0)
    return (growth[:, None] * push_term, inflow)

def ocean_step(sediment, above_rows, below_rows, flow_lo, flow_hi, flow_y, open_lo, open_hi, open_y, settle_rate, erosion_gain):
    right_cells = jnp.pad(sediment, ((0, 0), (0, 0), (0, 1)))[:, :, 1:]
    flux_lo = jnp.maximum(flow_lo, 0.0) * above_rows + jnp.minimum(flow_lo, 0.0) * sediment - KAPPA * open_lo * (sediment - above_rows)
    flux_hi = jnp.maximum(flow_hi, 0.0) * sediment + jnp.minimum(flow_hi, 0.0) * below_rows - KAPPA * open_hi * (below_rows - sediment)
    flux_y = jnp.maximum(flow_y, 0.0) * sediment + jnp.minimum(flow_y, 0.0) * right_cells - KAPPA * open_y * (right_cells - sediment)
    flux_left = jnp.pad(flux_y, ((0, 0), (0, 0), (1, 0)))[:, :, :-1]
    return sediment - (flux_hi - flux_lo) - (flux_y - flux_left) - settle_rate[:, None, None] * sediment + erosion_gain

def reference(ocean_conc, flow_lo, flow_hi, flow_y, open_lo, open_hi, open_y, settle_rate, critical_stress, erosion_rate, wave_energy, band_angle, band_speed, band_growth, band_orbital, neighbors, facing_angle, live_nodes, remap_owner, remap_slot, remap_cell, remap_weight):
    forcing, current_square = coupling_fields(flow_lo, flow_hi, flow_y)
    entry_count = PEERS * ENT
    source = jnp.arange(entry_count, dtype=jnp.int32) // ENT * OB_DEV + remap_cell
    target = remap_owner[:, 0] * WB_DEV + remap_slot
    weights = remap_weight.astype(jnp.float32)
    picked = jnp.transpose(forcing.reshape(4, PEERS * OB_DEV, 64)[:, source, :], (1, 0, 2))
    pieces = jnp.einsum('eji,eci->ecj', weights, picked, precision=HIGHEST).reshape(entry_count, 256)
    wave_blocks = jax.ops.segment_sum(pieces, target, num_segments=PEERS * WB_DEV)
    wave_forcing = jnp.transpose(wave_blocks.reshape(PEERS * WB_DEV, 4, 64), (1, 0, 2)).reshape(4, WNODES)
    alive_mask = live_nodes.astype(jnp.float32)[None, :]
    band_group = math.gcd(BANDS, 32)

    def wave_group(orbital, inputs):
        energy_in, band_dir, band_pace, growth, orbit_gain = inputs
        source_term, inflow = band_rates(wave_forcing, band_dir, band_pace, growth, facing_angle)
        total_rate = lax.optimization_barrier(jnp.sum(inflow, axis=0))
        energy = (energy_in.astype(jnp.float32) + source_term) * alive_mask
        for sweep in range(WSTEPS):
            arriving = jnp.zeros_like(energy)
            for neighbor in range(NBRS):
                arriving = arriving + inflow[neighbor] * energy[:, neighbors[neighbor]]
            energy = (energy + arriving - total_rate * energy) * alive_mask
        coefficient = jnp.stack([orbit_gain * jnp.cos(band_dir), orbit_gain * jnp.sin(band_dir)])
        orbital = orbital + jnp.dot(coefficient, energy, precision=HIGHEST)
        return (orbital, energy.astype(jnp.bfloat16))
    grouped = (wave_energy.reshape(BANDS // band_group, band_group, WNODES), band_angle.reshape(-1, band_group), band_speed.reshape(-1, band_group), band_growth.reshape(-1, band_group), band_orbital.reshape(-1, band_group))
    orbital, wave_rows = lax.scan(wave_group, jnp.zeros((2, WNODES), jnp.float32), grouped)
    waves_out = wave_rows.reshape(BANDS, WNODES)
    orbital_blocks = jnp.transpose(orbital.reshape(2, PEERS * WB_DEV, 64), (1, 0, 2))
    returned = orbital_blocks[target]
    spread = jnp.einsum('eji,ecj->eci', weights, returned, precision=HIGHEST).reshape(entry_count, 128)
    ocean_blocks = jax.ops.segment_sum(spread, source, num_segments=PEERS * OB_DEV)
    ocean_orbital = jnp.transpose(ocean_blocks.reshape(PEERS * OB_DEV, 2, 64), (1, 0, 2)).reshape(2, OX, OY)
    stress = TAU_CURRENT * current_square + TAU_WAVES * (ocean_orbital[0] * ocean_orbital[0] + ocean_orbital[1] * ocean_orbital[1])
    erosion_gain = erosion_rate[:, None, None] * jnp.maximum(stress[None] / critical_stress[:, None, None] - 1.0, 0.0)
    lower_flow = flow_lo.astype(jnp.float32)
    upper_flow = flow_hi.astype(jnp.float32)
    side_flow = flow_y.astype(jnp.float32)
    lower_open = open_lo.astype(jnp.float32)
    upper_open = open_hi.astype(jnp.float32)
    side_open = open_y.astype(jnp.float32)
    sediment = ocean_conc
    for sweep in range(OSTEPS):
        above_rows = jnp.pad(sediment, ((0, 0), (1, 0), (0, 0)))[:, :-1]
        below_rows = jnp.pad(sediment, ((0, 0), (0, 1), (0, 0)))[:, 1:]
        sediment = ocean_step(sediment, above_rows, below_rows, lower_flow, upper_flow, side_flow, lower_open, upper_open, side_open, settle_rate, erosion_gain)
    return (sediment, waves_out)
```

```python
import jax
import jax.numpy as jnp
from jax import lax
from jax.sharding import PartitionSpec as P

OSTEPS = 4
WSTEPS = 4
NBRS = 4


KAPPA = 0.07
FORCE_SCALE = 5.0
DRAG = 50.0
TAU_CURRENT = 20.0
TAU_WAVES = 10.0
HIGHEST = lax.Precision.HIGHEST


def with_halo(x, sides, width):
    for axis, dim in sides:
        count, length = (lax.axis_size(axis), x.shape[dim])
        up = [(i, (i + 1) % count) for i in range(count - 1)]
        down = [(j, i) for i, j in up]
        last = lax.slice_in_dim(x, length - width, length, axis=dim)
        first = lax.slice_in_dim(x, 0, width, axis=dim)
        before = lax.ppermute(last, axis, up)
        after = lax.ppermute(first, axis, down)
        x = jnp.concatenate([before, x, after], axis=dim)
    return x


def coupling_fields(flow_lo, flow_hi, flow_y):
    eastward = 0.5 * (flow_lo.astype(jnp.float32) + flow_hi.astype(jnp.float32))
    across = flow_y.astype(jnp.float32)
    earlier = jnp.pad(across, ((0, 0), (1, 0)))[:, :-1]
    northward = 0.5 * (across + earlier)
    current_speed = jnp.sqrt(eastward * eastward + northward * northward)
    forcing = jnp.stack(
        [
            FORCE_SCALE * eastward,
            FORCE_SCALE * northward,
            DRAG * current_speed * eastward,
            DRAG * current_speed * northward,
        ]
    )
    return (forcing, eastward * eastward + northward * northward)


def band_rates(wave_forcing, band_dir, band_pace, growth, facing):
    cosines = jnp.cos(band_dir)[:, None]
    sine_terms = jnp.sin(band_dir)[:, None]
    drift_term = cosines * wave_forcing[0][None, :] + sine_terms * wave_forcing[1][None, :]
    push_term = jnp.maximum(
        cosines * wave_forcing[2][None, :] + sine_terms * wave_forcing[3][None, :], 0.0
    )
    base_rate = 0.5 * band_pace[:, None] * (1.0 + 0.5 * jnp.tanh(drift_term))
    inflow = base_rate[None] * jnp.maximum(
        -jnp.cos(band_dir[None, :, None] - facing[:, None, :]), 0.0
    )
    return (growth[:, None] * push_term, inflow)


def ocean_step(
    sediment,
    above_rows,
    below_rows,
    flow_lo,
    flow_hi,
    flow_y,
    open_lo,
    open_hi,
    open_y,
    settle_rate,
    erosion_gain,
):
    right_cells = jnp.pad(sediment, ((0, 0), (0, 0), (0, 1)))[:, :, 1:]
    flux_lo = (
        jnp.maximum(flow_lo, 0.0) * above_rows
        + jnp.minimum(flow_lo, 0.0) * sediment
        - KAPPA * open_lo * (sediment - above_rows)
    )
    flux_hi = (
        jnp.maximum(flow_hi, 0.0) * sediment
        + jnp.minimum(flow_hi, 0.0) * below_rows
        - KAPPA * open_hi * (below_rows - sediment)
    )
    flux_y = (
        jnp.maximum(flow_y, 0.0) * sediment
        + jnp.minimum(flow_y, 0.0) * right_cells
        - KAPPA * open_y * (right_cells - sediment)
    )
    flux_left = jnp.pad(flux_y, ((0, 0), (0, 0), (1, 0)))[:, :, :-1]
    return (
        sediment
        - (flux_hi - flux_lo)
        - (flux_y - flux_left)
        - settle_rate[:, None, None] * sediment
        + erosion_gain
    )


def entry_rank(owners, peer_count):
    onehot = (owners[:, None] == jnp.arange(peer_count, dtype=jnp.int32)[None, :]).astype(jnp.int32)
    earlier = jnp.cumsum(onehot, axis=0) - onehot
    return jnp.sum(earlier * onehot, axis=1)


def per_device(
    ocean_conc,
    flow_lo,
    flow_hi,
    flow_y,
    open_lo,
    open_hi,
    open_y,
    settle_rate,
    critical_stress,
    erosion_rate,
    wave_energy,
    band_angle,
    band_speed,
    band_growth,
    band_orbital,
    neighbors,
    facing_angle,
    live_nodes,
    remap_owner,
    remap_slot,
    remap_cell,
    remap_weight,
):
    peer_count = lax.axis_size(("sec", "tile"))
    entry_count = remap_cell.shape[0]
    capacity = min(entry_count, max(2, 2 * entry_count // peer_count))
    slot_count = peer_count * capacity
    row_count, column_count = flow_lo.shape
    ocean_count = row_count * column_count // 64
    node_count = wave_energy.shape[1]
    block_count = node_count // 64
    forcing, current_square = coupling_fields(flow_lo, flow_hi, flow_y)
    weights = remap_weight.astype(jnp.float32)
    picked = jnp.transpose(forcing.reshape(4, ocean_count, 64)[:, remap_cell, :], (1, 0, 2))
    pieces = jnp.einsum("eji,eci->ecj", weights, picked, precision=HIGHEST).reshape(
        entry_count, 256
    )
    owners = remap_owner[:, 0]
    ranking = entry_rank(owners, peer_count)
    position = owners * capacity + ranking
    tagged = jnp.concatenate([pieces, remap_slot.astype(jnp.float32)[:, None]], axis=1)
    send_rows = jnp.full((slot_count, 257), -1.0, jnp.float32).at[position].set(tagged)
    got = lax.all_to_all(send_rows, ("sec", "tile"), split_axis=0, concat_axis=0, tiled=True)
    got_rows = got[:, :256]
    got_ids = got[:, 256].astype(jnp.int32)
    block_index = jnp.arange(block_count, dtype=jnp.int32)
    select = (got_ids[None, :] == block_index[:, None]).astype(jnp.float32)
    wave_blocks = jnp.dot(select, got_rows, precision=HIGHEST)
    wave_forcing = jnp.transpose(wave_blocks.reshape(block_count, 4, 64), (1, 0, 2)).reshape(
        4, node_count
    )
    alive_mask = live_nodes.astype(jnp.float32)[None, :]
    source_term, inflow = band_rates(
        wave_forcing, band_angle, band_speed, band_growth, facing_angle
    )
    energy = (wave_energy.astype(jnp.float32) + source_term) * alive_mask
    first_node = lax.axis_index(("sec", "tile")) * node_count
    total_rate = jnp.sum(inflow, axis=0)
    local_index = neighbors - first_node + 128
    for sweep in range(WSTEPS):
        padded = with_halo(energy, ((("sec", "tile"), 1),), 128)
        arriving = jnp.zeros_like(energy)
        for neighbor in range(NBRS):
            arriving = arriving + inflow[neighbor] * jnp.take(padded, local_index[neighbor], axis=1)
        energy = (energy + arriving - total_rate * energy) * alive_mask
    waves_out = energy.astype(jnp.bfloat16)
    coefficient = jnp.stack(
        [band_orbital * jnp.cos(band_angle), band_orbital * jnp.sin(band_angle)]
    )
    orbital = lax.psum(jnp.dot(coefficient, energy, precision=HIGHEST), "lev")
    orbital_blocks = jnp.transpose(orbital.reshape(2, block_count, 64), (1, 0, 2)).reshape(
        block_count, 128
    )
    back_rows = jnp.einsum("ws,wc->sc", select, orbital_blocks, precision=HIGHEST)
    returned = lax.all_to_all(back_rows, ("sec", "tile"), split_axis=0, concat_axis=0, tiled=True)
    mine = returned[position].reshape(entry_count, 2, 64)
    spread = jnp.einsum("eji,ecj->eci", weights, mine, precision=HIGHEST).reshape(entry_count, 128)
    ocean_select = (
        remap_cell[None, :] == jnp.arange(ocean_count, dtype=jnp.int32)[:, None]
    ).astype(jnp.float32)
    ocean_blocks = jnp.dot(ocean_select, spread, precision=HIGHEST)
    ocean_orbital = jnp.transpose(ocean_blocks.reshape(ocean_count, 2, 64), (1, 0, 2)).reshape(
        2, row_count, column_count
    )
    stress = TAU_CURRENT * current_square + TAU_WAVES * (
        ocean_orbital[0] * ocean_orbital[0] + ocean_orbital[1] * ocean_orbital[1]
    )
    erosion_gain = erosion_rate[:, None, None] * jnp.maximum(
        stress[None] / critical_stress[:, None, None] - 1.0, 0.0
    )
    classes = ocean_conc.shape[0]
    fields = jnp.concatenate(
        [
            ocean_conc,
            erosion_gain,
            jnp.stack(
                [
                    flow_lo.astype(jnp.float32),
                    flow_hi.astype(jnp.float32),
                    flow_y.astype(jnp.float32),
                    open_lo.astype(jnp.float32),
                    open_hi.astype(jnp.float32),
                    open_y.astype(jnp.float32),
                ]
            ),
        ]
    )
    wide = with_halo(fields, ((("sec", "tile"), 1),), OSTEPS)
    sediment = wide[:classes]
    gain = wide[classes : 2 * classes]
    lower_flow, upper_flow, side_flow, lower_open, upper_open, side_open = (
        wide[2 * classes + k] for k in range(6)
    )
    for sweep in range(OSTEPS):
        above_rows = jnp.pad(sediment, ((0, 0), (1, 0), (0, 0)))[:, :-1]
        below_rows = jnp.pad(sediment, ((0, 0), (0, 1), (0, 0)))[:, 1:]
        sediment = ocean_step(
            sediment,
            above_rows,
            below_rows,
            lower_flow,
            upper_flow,
            side_flow,
            lower_open,
            upper_open,
            side_open,
            settle_rate,
            gain,
        )
    sediment = sediment[:, OSTEPS : OSTEPS + row_count]
    return (sediment, waves_out)


def solution(mesh):
    return jax.shard_map(
        per_device,
        mesh=mesh,
        in_specs=(
            P("lev", ("sec", "tile"), None),
            P(("sec", "tile"), None),
            P(("sec", "tile"), None),
            P(("sec", "tile"), None),
            P(("sec", "tile"), None),
            P(("sec", "tile"), None),
            P(("sec", "tile"), None),
            P("lev"),
            P("lev"),
            P("lev"),
            P("lev", ("sec", "tile")),
            P("lev"),
            P("lev"),
            P("lev"),
            P("lev"),
            P(None, ("sec", "tile")),
            P(None, ("sec", "tile")),
            P(("sec", "tile")),
            P(("sec", "tile"), None),
            P(("sec", "tile")),
            P(("sec", "tile")),
            P(("sec", "tile"), None, None),
        ),
        out_specs=(P("lev", ("sec", "tile"), None), P("lev", ("sec", "tile"))),
        check_vma=False,
    )
```

```python
import jax
import jax.numpy as jnp
from jax import lax
from jax.experimental import pallas as pl
from jax.experimental.pallas import tpu as pltpu
from jax.sharding import PartitionSpec as P

OSTEPS = 4
WSTEPS = 4
NBRS = 4


KAPPA = 0.07
FORCE_SCALE = 5.0
DRAG = 50.0
TAU_CURRENT = 20.0
TAU_WAVES = 10.0
HIGHEST = lax.Precision.HIGHEST


def with_halo(x, sides, width):
    for axis, dim in sides:
        count, length = (lax.axis_size(axis), x.shape[dim])
        up = [(i, (i + 1) % count) for i in range(count - 1)]
        down = [(j, i) for i, j in up]
        last = lax.slice_in_dim(x, length - width, length, axis=dim)
        first = lax.slice_in_dim(x, 0, width, axis=dim)
        before = lax.ppermute(last, axis, up)
        after = lax.ppermute(first, axis, down)
        x = jnp.concatenate([before, x, after], axis=dim)
    return x


def coupling_fields(flow_lo, flow_hi, flow_y):
    eastward = 0.5 * (flow_lo.astype(jnp.float32) + flow_hi.astype(jnp.float32))
    across = flow_y.astype(jnp.float32)
    earlier = jnp.pad(across, ((0, 0), (1, 0)))[:, :-1]
    northward = 0.5 * (across + earlier)
    current_speed = jnp.sqrt(eastward * eastward + northward * northward)
    forcing = jnp.stack(
        [
            FORCE_SCALE * eastward,
            FORCE_SCALE * northward,
            DRAG * current_speed * eastward,
            DRAG * current_speed * northward,
        ]
    )
    return (forcing, eastward * eastward + northward * northward)


def band_rates(wave_forcing, band_dir, band_pace, growth, facing):
    cosines = jnp.cos(band_dir)[:, None]
    sine_terms = jnp.sin(band_dir)[:, None]
    drift_term = cosines * wave_forcing[0][None, :] + sine_terms * wave_forcing[1][None, :]
    push_term = jnp.maximum(
        cosines * wave_forcing[2][None, :] + sine_terms * wave_forcing[3][None, :], 0.0
    )
    base_rate = 0.5 * band_pace[:, None] * (1.0 + 0.5 * jnp.tanh(drift_term))
    facing_cos = jnp.cos(facing)[:, None, :]
    facing_sin = jnp.sin(facing)[:, None, :]
    along = cosines[None] * facing_cos + sine_terms[None] * facing_sin
    inflow = base_rate[None] * jnp.maximum(-along, 0.0)
    return (growth[:, None] * push_term, inflow)


def split3(x):
    hi = lax.reduce_precision(x, exponent_bits=8, mantissa_bits=7)
    rest = x - hi
    mid = lax.reduce_precision(rest, exponent_bits=8, mantissa_bits=7)
    lo = rest - mid
    return hi.astype(jnp.bfloat16), mid.astype(jnp.bfloat16), lo.astype(jnp.bfloat16)


def sweep_kernel(padded_ref, sel_ref, inflow_ref, rate_ref, alive_ref, out_ref):
    bands = out_ref.shape[0]
    for t in range(sel_ref.shape[0]):
        window = padded_ref[:, 128 * t : 128 * t + 384]
        parts = jnp.concatenate(split3(window), axis=0)
        picked = jnp.dot(parts, sel_ref[t], preferred_element_type=jnp.float32)
        gathered = picked[:bands] + picked[bands : 2 * bands] + picked[2 * bands :]
        cols = slice(128 * t, 128 * t + 128)
        energy = padded_ref[:, 128 * t + 128 : 128 * t + 256]
        arriving = inflow_ref[0, :, cols] * gathered[:, 0:128]
        for k in range(1, NBRS):
            arriving = arriving + inflow_ref[k, :, cols] * gathered[:, 128 * k : 128 * k + 128]
        out_ref[:, cols] = (energy + arriving - rate_ref[:, cols] * energy) * alive_ref[:, cols]


def wave_sweep(padded, sel, inflow, rate, alive):
    bands, nodes = rate.shape
    vmem = pl.BlockSpec(memory_space=pltpu.VMEM)
    flops = 2 * 3 * bands * 384 * nodes * NBRS
    moved = 4 * (padded.size + inflow.size + 2 * rate.size) + 2 * sel.size
    return pl.pallas_call(
        sweep_kernel,
        out_shape=jax.ShapeDtypeStruct((bands, nodes), jnp.float32),
        in_specs=[vmem] * 5,
        out_specs=vmem,
        cost_estimate=pl.CostEstimate(flops=flops, bytes_accessed=moved, transcendentals=0),
    )(padded, sel, inflow, rate, alive)


def selection(local_index):
    nbrs, nodes = local_index.shape
    tiles = nodes // 128
    start = 128 * jnp.arange(tiles, dtype=jnp.int32)
    idx = local_index.reshape(nbrs, tiles, 128) - start[None, :, None]
    rows = jnp.arange(384, dtype=jnp.int32)
    sel = idx.transpose(1, 0, 2)[:, None, :, :] == rows[None, :, None, None]
    return sel.reshape(tiles, 384, nbrs * 128).astype(jnp.bfloat16)


def lev_sum(x):
    count = lax.axis_size("lev")
    if count & (count - 1):
        return lax.psum(x, "lev")
    step = 1
    while step < count:
        x = x + lax.ppermute(x, "lev", [(i, i ^ step) for i in range(count)])
        step *= 2
    return x


def ocean_step(
    sediment,
    above_rows,
    below_rows,
    flow_lo,
    flow_hi,
    flow_y,
    open_lo,
    open_hi,
    open_y,
    settle_rate,
    erosion_gain,
):
    right_cells = jnp.pad(sediment, ((0, 0), (0, 0), (0, 1)))[:, :, 1:]
    flux_lo = (
        jnp.maximum(flow_lo, 0.0) * above_rows
        + jnp.minimum(flow_lo, 0.0) * sediment
        - KAPPA * open_lo * (sediment - above_rows)
    )
    flux_hi = (
        jnp.maximum(flow_hi, 0.0) * sediment
        + jnp.minimum(flow_hi, 0.0) * below_rows
        - KAPPA * open_hi * (below_rows - sediment)
    )
    flux_y = (
        jnp.maximum(flow_y, 0.0) * sediment
        + jnp.minimum(flow_y, 0.0) * right_cells
        - KAPPA * open_y * (right_cells - sediment)
    )
    flux_left = jnp.pad(flux_y, ((0, 0), (0, 0), (1, 0)))[:, :, :-1]
    return (
        sediment
        - (flux_hi - flux_lo)
        - (flux_y - flux_left)
        - settle_rate[:, None, None] * sediment
        + erosion_gain
    )


def entry_rank(owners, peer_count):
    onehot = (owners[:, None] == jnp.arange(peer_count, dtype=jnp.int32)[None, :]).astype(jnp.int32)
    earlier = jnp.cumsum(onehot, axis=0) - onehot
    return jnp.sum(earlier * onehot, axis=1)


def per_device(
    ocean_conc,
    flow_lo,
    flow_hi,
    flow_y,
    open_lo,
    open_hi,
    open_y,
    settle_rate,
    critical_stress,
    erosion_rate,
    wave_energy,
    band_angle,
    band_speed,
    band_growth,
    band_orbital,
    neighbors,
    facing_angle,
    live_nodes,
    remap_owner,
    remap_slot,
    remap_cell,
    remap_weight,
):
    peer_count = lax.axis_size(("sec", "tile"))
    entry_count = remap_cell.shape[0]
    capacity = min(entry_count, max(2, 2 * entry_count // peer_count))
    slot_count = peer_count * capacity
    row_count, column_count = flow_lo.shape
    ocean_count = row_count * column_count // 64
    node_count = wave_energy.shape[1]
    block_count = node_count // 64
    forcing, current_square = coupling_fields(flow_lo, flow_hi, flow_y)
    weights = remap_weight.astype(jnp.float32)
    picked = jnp.transpose(forcing.reshape(4, ocean_count, 64)[:, remap_cell, :], (1, 0, 2))
    pieces = jnp.einsum("eji,eci->ecj", weights, picked, precision=HIGHEST).reshape(
        entry_count, 256
    )
    owners = remap_owner[:, 0]
    ranking = entry_rank(owners, peer_count)
    position = owners * capacity + ranking
    tagged = jnp.concatenate([pieces, remap_slot.astype(jnp.float32)[:, None]], axis=1)
    send_rows = jnp.full((slot_count, 257), -1.0, jnp.float32).at[position].set(tagged)
    got = lax.all_to_all(send_rows, ("sec", "tile"), split_axis=0, concat_axis=0, tiled=True)
    got_rows = got[:, :256]
    got_ids = got[:, 256].astype(jnp.int32)
    block_index = jnp.arange(block_count, dtype=jnp.int32)
    select = (got_ids[None, :] == block_index[:, None]).astype(jnp.float32)
    wave_blocks = jnp.dot(select, got_rows, precision=HIGHEST)
    wave_forcing = jnp.transpose(wave_blocks.reshape(block_count, 4, 64), (1, 0, 2)).reshape(
        4, node_count
    )
    alive_mask = live_nodes.astype(jnp.float32)[None, :]
    source_term, inflow = band_rates(
        wave_forcing, band_angle, band_speed, band_growth, facing_angle
    )
    energy = (wave_energy.astype(jnp.float32) + source_term) * alive_mask
    first_node = lax.axis_index(("sec", "tile")) * node_count
    total_rate = jnp.sum(inflow, axis=0)
    local_index = neighbors - first_node + 128
    sel = selection(local_index)
    for sweep in range(WSTEPS):
        padded = with_halo(energy, ((("sec", "tile"), 1),), 128)
        energy = wave_sweep(padded, sel, inflow, total_rate, alive_mask)
    waves_out = energy.astype(jnp.bfloat16)
    coefficient = jnp.stack(
        [band_orbital * jnp.cos(band_angle), band_orbital * jnp.sin(band_angle)]
    )
    orbital = lev_sum(jnp.dot(coefficient, energy, precision=HIGHEST))
    orbital_blocks = jnp.transpose(orbital.reshape(2, block_count, 64), (1, 0, 2)).reshape(
        block_count, 128
    )
    back_rows = jnp.einsum("ws,wc->sc", select, orbital_blocks, precision=HIGHEST)
    returned = lax.all_to_all(back_rows, ("sec", "tile"), split_axis=0, concat_axis=0, tiled=True)
    mine = returned[position].reshape(entry_count, 2, 64)
    spread = jnp.einsum("eji,ecj->eci", weights, mine, precision=HIGHEST).reshape(entry_count, 128)
    ocean_select = (
        remap_cell[None, :] == jnp.arange(ocean_count, dtype=jnp.int32)[:, None]
    ).astype(jnp.float32)
    ocean_blocks = jnp.dot(ocean_select, spread, precision=HIGHEST)
    ocean_orbital = jnp.transpose(ocean_blocks.reshape(ocean_count, 2, 64), (1, 0, 2)).reshape(
        2, row_count, column_count
    )
    stress = TAU_CURRENT * current_square + TAU_WAVES * (
        ocean_orbital[0] * ocean_orbital[0] + ocean_orbital[1] * ocean_orbital[1]
    )
    erosion_gain = erosion_rate[:, None, None] * jnp.maximum(
        stress[None] / critical_stress[:, None, None] - 1.0, 0.0
    )
    classes = ocean_conc.shape[0]
    fields = jnp.concatenate(
        [
            ocean_conc,
            erosion_gain,
            jnp.stack(
                [
                    flow_lo.astype(jnp.float32),
                    flow_hi.astype(jnp.float32),
                    flow_y.astype(jnp.float32),
                    open_lo.astype(jnp.float32),
                    open_hi.astype(jnp.float32),
                    open_y.astype(jnp.float32),
                ]
            ),
        ]
    )
    wide = with_halo(fields, ((("sec", "tile"), 1),), OSTEPS)
    sediment = wide[:classes]
    gain = wide[classes : 2 * classes]
    lower_flow, upper_flow, side_flow, lower_open, upper_open, side_open = (
        wide[2 * classes + k] for k in range(6)
    )
    for sweep in range(OSTEPS):
        above_rows = jnp.pad(sediment, ((0, 0), (1, 0), (0, 0)))[:, :-1]
        below_rows = jnp.pad(sediment, ((0, 0), (0, 1), (0, 0)))[:, 1:]
        sediment = ocean_step(
            sediment,
            above_rows,
            below_rows,
            lower_flow,
            upper_flow,
            side_flow,
            lower_open,
            upper_open,
            side_open,
            settle_rate,
            gain,
        )
    sediment = sediment[:, OSTEPS : OSTEPS + row_count]
    return (sediment, waves_out)


def solution(mesh):
    return jax.shard_map(
        per_device,
        mesh=mesh,
        in_specs=(
            P("lev", ("sec", "tile"), None),
            P(("sec", "tile"), None),
            P(("sec", "tile"), None),
            P(("sec", "tile"), None),
            P(("sec", "tile"), None),
            P(("sec", "tile"), None),
            P(("sec", "tile"), None),
            P("lev"),
            P("lev"),
            P("lev"),
            P("lev", ("sec", "tile")),
            P("lev"),
            P("lev"),
            P("lev"),
            P("lev"),
            P(None, ("sec", "tile")),
            P(None, ("sec", "tile")),
            P(("sec", "tile")),
            P(("sec", "tile"), None),
            P(("sec", "tile")),
            P(("sec", "tile")),
            P(("sec", "tile"), None, None),
        ),
        out_specs=(P("lev", ("sec", "tile"), None), P("lev", ("sec", "tile"))),
        check_vma=False,
    )
```

```python
import jax
import jax.numpy as jnp
from jax import lax
from jax.experimental import pallas as pl
from jax.experimental.pallas import tpu as pltpu
from jax.sharding import PartitionSpec as P

OSTEPS = 4
WSTEPS = 4
NBRS = 4


KAPPA = 0.07
FORCE_SCALE = 5.0
DRAG = 50.0
TAU_CURRENT = 20.0
TAU_WAVES = 10.0
HIGHEST = lax.Precision.HIGHEST


def with_halo(x, sides, width):
    for axis, dim in sides:
        count, length = (lax.axis_size(axis), x.shape[dim])
        up = [(i, (i + 1) % count) for i in range(count - 1)]
        down = [(j, i) for i, j in up]
        last = lax.slice_in_dim(x, length - width, length, axis=dim)
        first = lax.slice_in_dim(x, 0, width, axis=dim)
        before = lax.ppermute(last, axis, up)
        after = lax.ppermute(first, axis, down)
        x = jnp.concatenate([before, x, after], axis=dim)
    return x


def coupling_fields(flow_lo, flow_hi, flow_y):
    eastward = 0.5 * (flow_lo.astype(jnp.float32) + flow_hi.astype(jnp.float32))
    across = flow_y.astype(jnp.float32)
    earlier = jnp.pad(across, ((0, 0), (1, 0)))[:, :-1]
    northward = 0.5 * (across + earlier)
    current_speed = jnp.sqrt(eastward * eastward + northward * northward)
    forcing = jnp.stack(
        [
            FORCE_SCALE * eastward,
            FORCE_SCALE * northward,
            DRAG * current_speed * eastward,
            DRAG * current_speed * northward,
        ]
    )
    return (forcing, eastward * eastward + northward * northward)


def band_rates(wave_forcing, band_dir, band_pace, growth, facing):
    cosines = jnp.cos(band_dir)[:, None]
    sine_terms = jnp.sin(band_dir)[:, None]
    drift_term = cosines * wave_forcing[0][None, :] + sine_terms * wave_forcing[1][None, :]
    push_term = jnp.maximum(
        cosines * wave_forcing[2][None, :] + sine_terms * wave_forcing[3][None, :], 0.0
    )
    base_rate = 0.5 * band_pace[:, None] * (1.0 + 0.5 * jnp.tanh(drift_term))
    facing_cos = jnp.cos(facing)[:, None, :]
    facing_sin = jnp.sin(facing)[:, None, :]
    along = cosines[None] * facing_cos + sine_terms[None] * facing_sin
    inflow = base_rate[None] * jnp.maximum(-along, 0.0)
    return (growth[:, None] * push_term, inflow)


def split3(x):
    hi = lax.reduce_precision(x, exponent_bits=8, mantissa_bits=7)
    rest = x - hi
    mid = lax.reduce_precision(rest, exponent_bits=8, mantissa_bits=7)
    lo = rest - mid
    return hi.astype(jnp.bfloat16), mid.astype(jnp.bfloat16), lo.astype(jnp.bfloat16)


def sweep_kernel(
    left_ref, energy_ref, right_ref, sel_ref, inflow_ref, rate_ref, alive_ref, out_ref, first_ref, last_ref
):
    bands = out_ref.shape[0]
    tiles = sel_ref.shape[0]
    blocks = (
        [left_ref[...]]
        + [energy_ref[:, 128 * t : 128 * t + 128] for t in range(tiles)]
        + [right_ref[...]]
    )
    for t in range(tiles):
        window = jnp.concatenate(blocks[t : t + 3], axis=1)
        parts = jnp.concatenate(split3(window), axis=0)
        picked = jnp.dot(parts, sel_ref[t], preferred_element_type=jnp.float32)
        gathered = picked[:bands] + picked[bands : 2 * bands] + picked[2 * bands :]
        cols = slice(128 * t, 128 * t + 128)
        energy = blocks[t + 1]
        arriving = inflow_ref[0, :, cols] * gathered[:, 0:128]
        for k in range(1, NBRS):
            arriving = arriving + inflow_ref[k, :, cols] * gathered[:, 128 * k : 128 * k + 128]
        fresh = (energy + arriving - rate_ref[:, cols] * energy) * alive_ref[:, cols]
        out_ref[:, cols] = fresh
        if t == 0:
            first_ref[...] = fresh
        if t == tiles - 1:
            last_ref[...] = fresh


def wave_sweep(left, energy, right, sel, inflow, rate, alive):
    bands, nodes = rate.shape
    vmem = pl.BlockSpec(memory_space=pltpu.VMEM)
    flops = 2 * 3 * bands * 384 * nodes * NBRS
    moved = 4 * (2 * left.size + inflow.size + 3 * rate.size) + 2 * sel.size
    edge = jax.ShapeDtypeStruct((bands, 128), jnp.float32)
    return pl.pallas_call(
        sweep_kernel,
        out_shape=(jax.ShapeDtypeStruct((bands, nodes), jnp.float32), edge, edge),
        in_specs=[vmem] * 7,
        out_specs=(vmem, vmem, vmem),
        cost_estimate=pl.CostEstimate(flops=flops, bytes_accessed=moved, transcendentals=0),
    )(left, energy, right, sel, inflow, rate, alive)


def selection(local_index):
    nbrs, nodes = local_index.shape
    tiles = nodes // 128
    start = 128 * jnp.arange(tiles, dtype=jnp.int32)
    idx = local_index.reshape(nbrs, tiles, 128) - start[None, :, None]
    rows = jnp.arange(384, dtype=jnp.int32)
    sel = idx.transpose(1, 0, 2)[:, None, :, :] == rows[None, :, None, None]
    return sel.reshape(tiles, 384, nbrs * 128).astype(jnp.bfloat16)


def ocean_step(
    sediment,
    above_rows,
    below_rows,
    flow_lo,
    flow_hi,
    flow_y,
    open_lo,
    open_hi,
    open_y,
    settle_rate,
    erosion_gain,
):
    right_cells = jnp.pad(sediment, ((0, 0), (0, 0), (0, 1)))[:, :, 1:]
    flux_lo = (
        jnp.maximum(flow_lo, 0.0) * above_rows
        + jnp.minimum(flow_lo, 0.0) * sediment
        - KAPPA * open_lo * (sediment - above_rows)
    )
    flux_hi = (
        jnp.maximum(flow_hi, 0.0) * sediment
        + jnp.minimum(flow_hi, 0.0) * below_rows
        - KAPPA * open_hi * (below_rows - sediment)
    )
    flux_y = (
        jnp.maximum(flow_y, 0.0) * sediment
        + jnp.minimum(flow_y, 0.0) * right_cells
        - KAPPA * open_y * (right_cells - sediment)
    )
    flux_left = jnp.pad(flux_y, ((0, 0), (0, 0), (1, 0)))[:, :, :-1]
    return (
        sediment
        - (flux_hi - flux_lo)
        - (flux_y - flux_left)
        - settle_rate[:, None, None] * sediment
        + erosion_gain
    )


def entry_rank(owners, peer_count):
    onehot = (owners[:, None] == jnp.arange(peer_count, dtype=jnp.int32)[None, :]).astype(jnp.int32)
    earlier = jnp.cumsum(onehot, axis=0) - onehot
    return jnp.sum(earlier * onehot, axis=1)


def per_device(
    ocean_conc,
    flow_lo,
    flow_hi,
    flow_y,
    open_lo,
    open_hi,
    open_y,
    settle_rate,
    critical_stress,
    erosion_rate,
    wave_energy,
    band_angle,
    band_speed,
    band_growth,
    band_orbital,
    neighbors,
    facing_angle,
    live_nodes,
    remap_owner,
    remap_slot,
    remap_cell,
    remap_weight,
):
    peer_count = lax.axis_size(("sec", "tile"))
    entry_count = remap_cell.shape[0]
    capacity = min(entry_count, max(2, 2 * entry_count // peer_count))
    slot_count = peer_count * capacity
    row_count, column_count = flow_lo.shape
    ocean_count = row_count * column_count // 64
    node_count = wave_energy.shape[1]
    block_count = node_count // 64
    forcing, current_square = coupling_fields(flow_lo, flow_hi, flow_y)
    weights = remap_weight.astype(jnp.float32)
    picked = jnp.transpose(forcing.reshape(4, ocean_count, 64)[:, remap_cell, :], (1, 0, 2))
    pieces = jnp.einsum("eji,eci->ecj", weights, picked, precision=HIGHEST).reshape(
        entry_count, 256
    )
    owners = remap_owner[:, 0]
    ranking = entry_rank(owners, peer_count)
    position = owners * capacity + ranking
    tagged = jnp.concatenate([pieces, remap_slot.astype(jnp.float32)[:, None]], axis=1)
    send_rows = jnp.full((slot_count, 257), -1.0, jnp.float32).at[position].set(tagged)
    got = lax.all_to_all(send_rows, ("sec", "tile"), split_axis=0, concat_axis=0, tiled=True)
    got_rows = got[:, :256]
    got_ids = got[:, 256].astype(jnp.int32)
    block_index = jnp.arange(block_count, dtype=jnp.int32)
    select = (got_ids[None, :] == block_index[:, None]).astype(jnp.float32)
    wave_blocks = jnp.dot(select, got_rows, precision=HIGHEST)
    wave_forcing = jnp.transpose(wave_blocks.reshape(block_count, 4, 64), (1, 0, 2)).reshape(
        4, node_count
    )
    alive_mask = live_nodes.astype(jnp.float32)[None, :]
    source_term, inflow = band_rates(
        wave_forcing, band_angle, band_speed, band_growth, facing_angle
    )
    energy = (wave_energy.astype(jnp.float32) + source_term) * alive_mask
    first_node = lax.axis_index(("sec", "tile")) * node_count
    total_rate = jnp.sum(inflow, axis=0)
    local_index = neighbors - first_node + 128
    sel = selection(local_index)
    wave_axis = ("sec", "tile")
    up = [(i, i + 1) for i in range(lax.axis_size(wave_axis) - 1)]
    down = [(j, i) for i, j in up]
    first, last = energy[:, :128], energy[:, -128:]
    for sweep in range(WSTEPS):
        left = lax.ppermute(last, wave_axis, up)
        right = lax.ppermute(first, wave_axis, down)
        energy, first, last = wave_sweep(left, energy, right, sel, inflow, total_rate, alive_mask)
    waves_out = energy.astype(jnp.bfloat16)
    coefficient = jnp.stack(
        [band_orbital * jnp.cos(band_angle), band_orbital * jnp.sin(band_angle)]
    )
    orbital = lax.psum(jnp.dot(coefficient, energy, precision=HIGHEST), "lev")
    orbital_blocks = jnp.transpose(orbital.reshape(2, block_count, 64), (1, 0, 2)).reshape(
        block_count, 128
    )
    back_rows = jnp.einsum("ws,wc->sc", select, orbital_blocks, precision=HIGHEST)
    returned = lax.all_to_all(back_rows, ("sec", "tile"), split_axis=0, concat_axis=0, tiled=True)
    mine = returned[position].reshape(entry_count, 2, 64)
    spread = jnp.einsum("eji,ecj->eci", weights, mine, precision=HIGHEST).reshape(entry_count, 128)
    ocean_select = (
        remap_cell[None, :] == jnp.arange(ocean_count, dtype=jnp.int32)[:, None]
    ).astype(jnp.float32)
    ocean_blocks = jnp.dot(ocean_select, spread, precision=HIGHEST)
    ocean_orbital = jnp.transpose(ocean_blocks.reshape(ocean_count, 2, 64), (1, 0, 2)).reshape(
        2, row_count, column_count
    )
    stress = TAU_CURRENT * current_square + TAU_WAVES * (
        ocean_orbital[0] * ocean_orbital[0] + ocean_orbital[1] * ocean_orbital[1]
    )
    erosion_gain = erosion_rate[:, None, None] * jnp.maximum(
        stress[None] / critical_stress[:, None, None] - 1.0, 0.0
    )
    classes = ocean_conc.shape[0]
    fields = jnp.concatenate(
        [
            ocean_conc,
            erosion_gain,
            jnp.stack(
                [
                    flow_lo.astype(jnp.float32),
                    flow_hi.astype(jnp.float32),
                    flow_y.astype(jnp.float32),
                    open_lo.astype(jnp.float32),
                    open_hi.astype(jnp.float32),
                    open_y.astype(jnp.float32),
                ]
            ),
        ]
    )
    wide = with_halo(fields, ((("sec", "tile"), 1),), OSTEPS)
    sediment = wide[:classes]
    gain = wide[classes : 2 * classes]
    lower_flow, upper_flow, side_flow, lower_open, upper_open, side_open = (
        wide[2 * classes + k] for k in range(6)
    )
    for sweep in range(OSTEPS):
        above_rows = jnp.pad(sediment, ((0, 0), (1, 0), (0, 0)))[:, :-1]
        below_rows = jnp.pad(sediment, ((0, 0), (0, 1), (0, 0)))[:, 1:]
        sediment = ocean_step(
            sediment,
            above_rows,
            below_rows,
            lower_flow,
            upper_flow,
            side_flow,
            lower_open,
            upper_open,
            side_open,
            settle_rate,
            gain,
        )
    sediment = sediment[:, OSTEPS : OSTEPS + row_count]
    return (sediment, waves_out)


def solution(mesh):
    return jax.shard_map(
        per_device,
        mesh=mesh,
        in_specs=(
            P("lev", ("sec", "tile"), None),
            P(("sec", "tile"), None),
            P(("sec", "tile"), None),
            P(("sec", "tile"), None),
            P(("sec", "tile"), None),
            P(("sec", "tile"), None),
            P(("sec", "tile"), None),
            P("lev"),
            P("lev"),
            P("lev"),
            P("lev", ("sec", "tile")),
            P("lev"),
            P("lev"),
            P("lev"),
            P("lev"),
            P(None, ("sec", "tile")),
            P(None, ("sec", "tile")),
            P(("sec", "tile")),
            P(("sec", "tile"), None),
            P(("sec", "tile")),
            P(("sec", "tile")),
            P(("sec", "tile"), None, None),
        ),
        out_specs=(P("lev", ("sec", "tile"), None), P("lev", ("sec", "tile"))),
        check_vma=False,
    )
```

```python
import jax
import jax.numpy as jnp
from jax import lax
from jax.experimental import pallas as pl
from jax.experimental.pallas import tpu as pltpu
from jax.sharding import PartitionSpec as P

OSTEPS = 4
WSTEPS = 4
NBRS = 4


KAPPA = 0.07
FORCE_SCALE = 5.0
DRAG = 50.0
TAU_CURRENT = 20.0
TAU_WAVES = 10.0
HIGHEST = lax.Precision.HIGHEST


def with_halo(x, sides, width):
    for axis, dim in sides:
        count, length = (lax.axis_size(axis), x.shape[dim])
        up = [(i, (i + 1) % count) for i in range(count - 1)]
        down = [(j, i) for i, j in up]
        last = lax.slice_in_dim(x, length - width, length, axis=dim)
        first = lax.slice_in_dim(x, 0, width, axis=dim)
        before = lax.ppermute(last, axis, up)
        after = lax.ppermute(first, axis, down)
        x = jnp.concatenate([before, x, after], axis=dim)
    return x


def coupling_fields(flow_lo, flow_hi, flow_y):
    eastward = 0.5 * (flow_lo.astype(jnp.float32) + flow_hi.astype(jnp.float32))
    across = flow_y.astype(jnp.float32)
    earlier = jnp.pad(across, ((0, 0), (1, 0)))[:, :-1]
    northward = 0.5 * (across + earlier)
    current_speed = jnp.sqrt(eastward * eastward + northward * northward)
    forcing = jnp.stack(
        [
            FORCE_SCALE * eastward,
            FORCE_SCALE * northward,
            DRAG * current_speed * eastward,
            DRAG * current_speed * northward,
        ]
    )
    return (forcing, eastward * eastward + northward * northward)


def band_rates(wave_forcing, band_dir, band_pace, growth, facing):
    cosines = jnp.cos(band_dir)[:, None]
    sine_terms = jnp.sin(band_dir)[:, None]
    drift_term = cosines * wave_forcing[0][None, :] + sine_terms * wave_forcing[1][None, :]
    push_term = jnp.maximum(
        cosines * wave_forcing[2][None, :] + sine_terms * wave_forcing[3][None, :], 0.0
    )
    base_rate = 0.5 * band_pace[:, None] * (1.0 + 0.5 * jnp.tanh(drift_term))
    facing_cos = jnp.cos(facing)[:, None, :]
    facing_sin = jnp.sin(facing)[:, None, :]
    along = cosines[None] * facing_cos + sine_terms[None] * facing_sin
    inflow = base_rate[None] * jnp.maximum(-along, 0.0)
    return (growth[:, None] * push_term, inflow)


def split3(x):
    hi = lax.reduce_precision(x, exponent_bits=8, mantissa_bits=7)
    rest = x - hi
    mid = lax.reduce_precision(rest, exponent_bits=8, mantissa_bits=7)
    lo = rest - mid
    return hi.astype(jnp.bfloat16), mid.astype(jnp.bfloat16), lo.astype(jnp.bfloat16)


def sweep_kernel(
    left_ref, energy_ref, right_ref, sel_ref, inflow_ref, rate_ref, alive_ref, out_ref, first_ref, last_ref
):
    bands = out_ref.shape[0]
    tiles = sel_ref.shape[0]
    blocks = (
        [left_ref[...]]
        + [energy_ref[:, 128 * t : 128 * t + 128] for t in range(tiles)]
        + [right_ref[...]]
    )
    pieces = [split3(block) for block in blocks]
    for t in range(tiles):
        parts = jnp.concatenate(
            [jnp.concatenate([pieces[t + b][p] for b in range(3)], axis=1) for p in range(3)],
            axis=0,
        )
        picked = jnp.dot(parts, sel_ref[t], preferred_element_type=jnp.float32)
        gathered = picked[:bands] + picked[bands : 2 * bands] + picked[2 * bands :]
        cols = slice(128 * t, 128 * t + 128)
        energy = blocks[t + 1]
        arriving = inflow_ref[0, :, cols] * gathered[:, 0:128]
        for k in range(1, NBRS):
            arriving = arriving + inflow_ref[k, :, cols] * gathered[:, 128 * k : 128 * k + 128]
        fresh = (energy + arriving - rate_ref[:, cols] * energy) * alive_ref[:, cols]
        out_ref[:, cols] = fresh
        if t == 0:
            first_ref[...] = fresh
        if t == tiles - 1:
            last_ref[...] = fresh


def wave_sweep(left, energy, right, sel, inflow, rate, alive):
    bands, nodes = rate.shape
    vmem = pl.BlockSpec(memory_space=pltpu.VMEM)
    flops = 2 * 3 * bands * 384 * nodes * NBRS
    moved = 4 * (2 * left.size + inflow.size + 3 * rate.size) + 2 * sel.size
    edge = jax.ShapeDtypeStruct((bands, 128), jnp.float32)
    return pl.pallas_call(
        sweep_kernel,
        out_shape=(jax.ShapeDtypeStruct((bands, nodes), jnp.float32), edge, edge),
        in_specs=[vmem] * 7,
        out_specs=(vmem, vmem, vmem),
        cost_estimate=pl.CostEstimate(flops=flops, bytes_accessed=moved, transcendentals=0),
    )(left, energy, right, sel, inflow, rate, alive)


def selection(local_index):
    nbrs, nodes = local_index.shape
    tiles = nodes // 128
    start = 128 * jnp.arange(tiles, dtype=jnp.int32)
    idx = local_index.reshape(nbrs, tiles, 128) - start[None, :, None]
    rows = jnp.arange(384, dtype=jnp.int32)
    sel = idx.transpose(1, 0, 2)[:, None, :, :] == rows[None, :, None, None]
    return sel.reshape(tiles, 384, nbrs * 128).astype(jnp.bfloat16)


def ocean_step(
    sediment,
    above_rows,
    below_rows,
    flow_lo,
    flow_hi,
    flow_y,
    open_lo,
    open_hi,
    open_y,
    settle_rate,
    erosion_gain,
):
    right_cells = jnp.pad(sediment, ((0, 0), (0, 0), (0, 1)))[:, :, 1:]
    flux_lo = (
        jnp.maximum(flow_lo, 0.0) * above_rows
        + jnp.minimum(flow_lo, 0.0) * sediment
        - KAPPA * open_lo * (sediment - above_rows)
    )
    flux_hi = (
        jnp.maximum(flow_hi, 0.0) * sediment
        + jnp.minimum(flow_hi, 0.0) * below_rows
        - KAPPA * open_hi * (below_rows - sediment)
    )
    flux_y = (
        jnp.maximum(flow_y, 0.0) * sediment
        + jnp.minimum(flow_y, 0.0) * right_cells
        - KAPPA * open_y * (right_cells - sediment)
    )
    flux_left = jnp.pad(flux_y, ((0, 0), (0, 0), (1, 0)))[:, :, :-1]
    return (
        sediment
        - (flux_hi - flux_lo)
        - (flux_y - flux_left)
        - settle_rate[:, None, None] * sediment
        + erosion_gain
    )


def entry_rank(owners, peer_count):
    onehot = (owners[:, None] == jnp.arange(peer_count, dtype=jnp.int32)[None, :]).astype(jnp.int32)
    earlier = jnp.cumsum(onehot, axis=0) - onehot
    return jnp.sum(earlier * onehot, axis=1)


def per_device(
    ocean_conc,
    flow_lo,
    flow_hi,
    flow_y,
    open_lo,
    open_hi,
    open_y,
    settle_rate,
    critical_stress,
    erosion_rate,
    wave_energy,
    band_angle,
    band_speed,
    band_growth,
    band_orbital,
    neighbors,
    facing_angle,
    live_nodes,
    remap_owner,
    remap_slot,
    remap_cell,
    remap_weight,
):
    peer_count = lax.axis_size(("sec", "tile"))
    entry_count = remap_cell.shape[0]
    capacity = min(entry_count, max(2, 2 * entry_count // peer_count))
    slot_count = peer_count * capacity
    row_count, column_count = flow_lo.shape
    ocean_count = row_count * column_count // 64
    node_count = wave_energy.shape[1]
    block_count = node_count // 64
    forcing, current_square = coupling_fields(flow_lo, flow_hi, flow_y)
    weights = remap_weight.astype(jnp.float32)
    picked = jnp.transpose(forcing.reshape(4, ocean_count, 64)[:, remap_cell, :], (1, 0, 2))
    pieces = jnp.einsum("eji,eci->ecj", weights, picked, precision=HIGHEST).reshape(
        entry_count, 256
    )
    owners = remap_owner[:, 0]
    ranking = entry_rank(owners, peer_count)
    position = owners * capacity + ranking
    tagged = jnp.concatenate([pieces, remap_slot.astype(jnp.float32)[:, None]], axis=1)
    send_rows = jnp.full((slot_count, 257), -1.0, jnp.float32).at[position].set(tagged)
    got = lax.all_to_all(send_rows, ("sec", "tile"), split_axis=0, concat_axis=0, tiled=True)
    got_rows = got[:, :256]
    got_ids = got[:, 256].astype(jnp.int32)
    block_index = jnp.arange(block_count, dtype=jnp.int32)
    select = (got_ids[None, :] == block_index[:, None]).astype(jnp.float32)
    wave_blocks = jnp.dot(select, got_rows, precision=HIGHEST)
    wave_forcing = jnp.transpose(wave_blocks.reshape(block_count, 4, 64), (1, 0, 2)).reshape(
        4, node_count
    )
    alive_mask = live_nodes.astype(jnp.float32)[None, :]
    source_term, inflow = band_rates(
        wave_forcing, band_angle, band_speed, band_growth, facing_angle
    )
    energy = (wave_energy.astype(jnp.float32) + source_term) * alive_mask
    first_node = lax.axis_index(("sec", "tile")) * node_count
    total_rate = jnp.sum(inflow, axis=0)
    local_index = neighbors - first_node + 128
    sel = selection(local_index)
    wave_axis = ("sec", "tile")
    up = [(i, i + 1) for i in range(lax.axis_size(wave_axis) - 1)]
    down = [(j, i) for i, j in up]
    first, last = energy[:, :128], energy[:, -128:]
    for sweep in range(WSTEPS):
        left = lax.ppermute(last, wave_axis, up)
        right = lax.ppermute(first, wave_axis, down)
        energy, first, last = wave_sweep(left, energy, right, sel, inflow, total_rate, alive_mask)
    waves_out = energy.astype(jnp.bfloat16)
    coefficient = jnp.stack(
        [band_orbital * jnp.cos(band_angle), band_orbital * jnp.sin(band_angle)]
    )
    orbital = lax.psum(jnp.dot(coefficient, energy, precision=HIGHEST), "lev")
    orbital_blocks = jnp.transpose(orbital.reshape(2, block_count, 64), (1, 0, 2)).reshape(
        block_count, 128
    )
    back_rows = jnp.einsum("ws,wc->sc", select, orbital_blocks, precision=HIGHEST)
    returned = lax.all_to_all(back_rows, ("sec", "tile"), split_axis=0, concat_axis=0, tiled=True)
    mine = returned[position].reshape(entry_count, 2, 64)
    spread = jnp.einsum("eji,ecj->eci", weights, mine, precision=HIGHEST).reshape(entry_count, 128)
    ocean_select = (
        remap_cell[None, :] == jnp.arange(ocean_count, dtype=jnp.int32)[:, None]
    ).astype(jnp.float32)
    ocean_blocks = jnp.dot(ocean_select, spread, precision=HIGHEST)
    ocean_orbital = jnp.transpose(ocean_blocks.reshape(ocean_count, 2, 64), (1, 0, 2)).reshape(
        2, row_count, column_count
    )
    stress = TAU_CURRENT * current_square + TAU_WAVES * (
        ocean_orbital[0] * ocean_orbital[0] + ocean_orbital[1] * ocean_orbital[1]
    )
    erosion_gain = erosion_rate[:, None, None] * jnp.maximum(
        stress[None] / critical_stress[:, None, None] - 1.0, 0.0
    )
    classes = ocean_conc.shape[0]
    fields = jnp.concatenate(
        [
            ocean_conc,
            erosion_gain,
            jnp.stack(
                [
                    flow_lo.astype(jnp.float32),
                    flow_hi.astype(jnp.float32),
                    flow_y.astype(jnp.float32),
                    open_lo.astype(jnp.float32),
                    open_hi.astype(jnp.float32),
                    open_y.astype(jnp.float32),
                ]
            ),
        ]
    )
    wide = with_halo(fields, ((("sec", "tile"), 1),), OSTEPS)
    sediment = wide[:classes]
    gain = wide[classes : 2 * classes]
    lower_flow, upper_flow, side_flow, lower_open, upper_open, side_open = (
        wide[2 * classes + k] for k in range(6)
    )
    for sweep in range(OSTEPS):
        above_rows = jnp.pad(sediment, ((0, 0), (1, 0), (0, 0)))[:, :-1]
        below_rows = jnp.pad(sediment, ((0, 0), (0, 1), (0, 0)))[:, 1:]
        sediment = ocean_step(
            sediment,
            above_rows,
            below_rows,
            lower_flow,
            upper_flow,
            side_flow,
            lower_open,
            upper_open,
            side_open,
            settle_rate,
            gain,
        )
    sediment = sediment[:, OSTEPS : OSTEPS + row_count]
    return (sediment, waves_out)


def solution(mesh):
    return jax.shard_map(
        per_device,
        mesh=mesh,
        in_specs=(
            P("lev", ("sec", "tile"), None),
            P(("sec", "tile"), None),
            P(("sec", "tile"), None),
            P(("sec", "tile"), None),
            P(("sec", "tile"), None),
            P(("sec", "tile"), None),
            P(("sec", "tile"), None),
            P("lev"),
            P("lev"),
            P("lev"),
            P("lev", ("sec", "tile")),
            P("lev"),
            P("lev"),
            P("lev"),
            P("lev"),
            P(None, ("sec", "tile")),
            P(None, ("sec", "tile")),
            P(("sec", "tile")),
            P(("sec", "tile"), None),
            P(("sec", "tile")),
            P(("sec", "tile")),
            P(("sec", "tile"), None, None),
        ),
        out_specs=(P("lev", ("sec", "tile"), None), P("lev", ("sec", "tile"))),
        check_vma=False,
    )
```

```python
import jax
import jax.numpy as jnp
from jax import lax
from jax.experimental import pallas as pl
from jax.experimental.pallas import tpu as pltpu
from jax.sharding import PartitionSpec as P

OSTEPS = 4
WSTEPS = 4
NBRS = 4


KAPPA = 0.07
FORCE_SCALE = 5.0
DRAG = 50.0
TAU_CURRENT = 20.0
TAU_WAVES = 10.0
HIGHEST = lax.Precision.HIGHEST


def with_halo(x, sides, width):
    for axis, dim in sides:
        count, length = (lax.axis_size(axis), x.shape[dim])
        up = [(i, (i + 1) % count) for i in range(count - 1)]
        down = [(j, i) for i, j in up]
        last = lax.slice_in_dim(x, length - width, length, axis=dim)
        first = lax.slice_in_dim(x, 0, width, axis=dim)
        before = lax.ppermute(last, axis, up)
        after = lax.ppermute(first, axis, down)
        x = jnp.concatenate([before, x, after], axis=dim)
    return x


def coupling_fields(flow_lo, flow_hi, flow_y):
    eastward = 0.5 * (flow_lo.astype(jnp.float32) + flow_hi.astype(jnp.float32))
    across = flow_y.astype(jnp.float32)
    earlier = jnp.pad(across, ((0, 0), (1, 0)))[:, :-1]
    northward = 0.5 * (across + earlier)
    current_speed = jnp.sqrt(eastward * eastward + northward * northward)
    forcing = jnp.stack(
        [
            FORCE_SCALE * eastward,
            FORCE_SCALE * northward,
            DRAG * current_speed * eastward,
            DRAG * current_speed * northward,
        ]
    )
    return (forcing, eastward * eastward + northward * northward)


def band_rates(wave_forcing, band_dir, band_pace, growth, facing):
    cosines = jnp.cos(band_dir)[:, None]
    sine_terms = jnp.sin(band_dir)[:, None]
    drift_term = cosines * wave_forcing[0][None, :] + sine_terms * wave_forcing[1][None, :]
    push_term = jnp.maximum(
        cosines * wave_forcing[2][None, :] + sine_terms * wave_forcing[3][None, :], 0.0
    )
    base_rate = 0.5 * band_pace[:, None] * (1.0 + 0.5 * jnp.tanh(drift_term))
    facing_cos = jnp.cos(facing)[:, None, :]
    facing_sin = jnp.sin(facing)[:, None, :]
    along = cosines[None] * facing_cos + sine_terms[None] * facing_sin
    inflow = base_rate[None] * jnp.maximum(-along, 0.0)
    return (growth[:, None] * push_term, inflow)


def split3(x):
    hi = lax.reduce_precision(x, exponent_bits=8, mantissa_bits=7)
    rest = x - hi
    mid = lax.reduce_precision(rest, exponent_bits=8, mantissa_bits=7)
    lo = rest - mid
    return hi.astype(jnp.bfloat16), mid.astype(jnp.bfloat16), lo.astype(jnp.bfloat16)


def sweep_kernel(
    left_ref,
    energy_ref,
    right_ref,
    sel_ref,
    inflow_ref,
    rate_ref,
    alive_ref,
    out_ref,
    first_ref,
    last_ref,
    ext_ref,
):
    bands = out_ref.shape[0]
    t = pl.program_id(0)
    tiles = pl.num_programs(0)
    nodes = energy_ref.shape[1]

    @pl.when(t == 0)
    def _():
        ext_ref[:, 0:128] = left_ref[...]
        ext_ref[:, 128 : 128 + nodes] = energy_ref[...]
        ext_ref[:, 128 + nodes : 256 + nodes] = right_ref[...]

    start = pl.multiple_of(t * 128, 128)
    window = ext_ref[:, pl.ds(start, 384)]
    parts = jnp.concatenate(split3(window), axis=0)
    picked = jnp.dot(parts, sel_ref[0], preferred_element_type=jnp.float32)
    gathered = picked[:bands] + picked[bands : 2 * bands] + picked[2 * bands :]
    energy = window[:, 128:256]
    arriving = inflow_ref[0] * gathered[:, 0:128]
    for k in range(1, NBRS):
        arriving = arriving + inflow_ref[k] * gathered[:, 128 * k : 128 * k + 128]
    fresh = (energy + arriving - rate_ref[...] * energy) * alive_ref[...]
    out_ref[...] = fresh

    @pl.when(t == 0)
    def _():
        first_ref[...] = fresh

    @pl.when(t == tiles - 1)
    def _():
        last_ref[...] = fresh


def wave_sweep(left, energy, right, sel, inflow, rate, alive):
    bands, nodes = rate.shape
    tiles = nodes // 128
    flops = 2 * 3 * bands * 384 * nodes * NBRS
    moved = 4 * (2 * left.size + inflow.size + 3 * rate.size) + 2 * sel.size
    edge = jax.ShapeDtypeStruct((bands, 128), jnp.float32)
    whole = lambda shape: pl.BlockSpec(shape, lambda t: (0,) * len(shape))
    return pl.pallas_call(
        sweep_kernel,
        grid=(tiles,),
        out_shape=(jax.ShapeDtypeStruct((bands, nodes), jnp.float32), edge, edge),
        in_specs=[
            whole((bands, 128)),
            whole((bands, nodes)),
            whole((bands, 128)),
            pl.BlockSpec((1, 384, NBRS * 128), lambda t: (t, 0, 0)),
            pl.BlockSpec((NBRS, bands, 128), lambda t: (0, 0, t)),
            pl.BlockSpec((bands, 128), lambda t: (0, t)),
            pl.BlockSpec((1, 128), lambda t: (0, t)),
        ],
        out_specs=(
            pl.BlockSpec((bands, 128), lambda t: (0, t)),
            whole((bands, 128)),
            whole((bands, 128)),
        ),
        scratch_shapes=[pltpu.VMEM((bands, nodes + 256), jnp.float32)],
        compiler_params=pltpu.CompilerParams(dimension_semantics=("arbitrary",)),
        cost_estimate=pl.CostEstimate(flops=flops, bytes_accessed=moved, transcendentals=0),
    )(left, energy, right, sel, inflow, rate, alive)


def selection(local_index):
    nbrs, nodes = local_index.shape
    tiles = nodes // 128
    start = 128 * jnp.arange(tiles, dtype=jnp.int32)
    idx = local_index.reshape(nbrs, tiles, 128) - start[None, :, None]
    rows = jnp.arange(384, dtype=jnp.int32)
    sel = idx.transpose(1, 0, 2)[:, None, :, :] == rows[None, :, None, None]
    return sel.reshape(tiles, 384, nbrs * 128).astype(jnp.bfloat16)


def ocean_step(
    sediment,
    above_rows,
    below_rows,
    flow_lo,
    flow_hi,
    flow_y,
    open_lo,
    open_hi,
    open_y,
    settle_rate,
    erosion_gain,
):
    right_cells = jnp.pad(sediment, ((0, 0), (0, 0), (0, 1)))[:, :, 1:]
    flux_lo = (
        jnp.maximum(flow_lo, 0.0) * above_rows
        + jnp.minimum(flow_lo, 0.0) * sediment
        - KAPPA * open_lo * (sediment - above_rows)
    )
    flux_hi = (
        jnp.maximum(flow_hi, 0.0) * sediment
        + jnp.minimum(flow_hi, 0.0) * below_rows
        - KAPPA * open_hi * (below_rows - sediment)
    )
    flux_y = (
        jnp.maximum(flow_y, 0.0) * sediment
        + jnp.minimum(flow_y, 0.0) * right_cells
        - KAPPA * open_y * (right_cells - sediment)
    )
    flux_left = jnp.pad(flux_y, ((0, 0), (0, 0), (1, 0)))[:, :, :-1]
    return (
        sediment
        - (flux_hi - flux_lo)
        - (flux_y - flux_left)
        - settle_rate[:, None, None] * sediment
        + erosion_gain
    )


def entry_rank(owners, peer_count):
    onehot = (owners[:, None] == jnp.arange(peer_count, dtype=jnp.int32)[None, :]).astype(jnp.int32)
    earlier = jnp.cumsum(onehot, axis=0) - onehot
    return jnp.sum(earlier * onehot, axis=1)


def per_device(
    ocean_conc,
    flow_lo,
    flow_hi,
    flow_y,
    open_lo,
    open_hi,
    open_y,
    settle_rate,
    critical_stress,
    erosion_rate,
    wave_energy,
    band_angle,
    band_speed,
    band_growth,
    band_orbital,
    neighbors,
    facing_angle,
    live_nodes,
    remap_owner,
    remap_slot,
    remap_cell,
    remap_weight,
):
    peer_count = lax.axis_size(("sec", "tile"))
    entry_count = remap_cell.shape[0]
    capacity = min(entry_count, max(2, 2 * entry_count // peer_count))
    slot_count = peer_count * capacity
    row_count, column_count = flow_lo.shape
    ocean_count = row_count * column_count // 64
    node_count = wave_energy.shape[1]
    block_count = node_count // 64
    forcing, current_square = coupling_fields(flow_lo, flow_hi, flow_y)
    weights = remap_weight.astype(jnp.float32)
    picked = jnp.transpose(forcing.reshape(4, ocean_count, 64)[:, remap_cell, :], (1, 0, 2))
    pieces = jnp.einsum("eji,eci->ecj", weights, picked, precision=HIGHEST).reshape(
        entry_count, 256
    )
    owners = remap_owner[:, 0]
    ranking = entry_rank(owners, peer_count)
    position = owners * capacity + ranking
    tagged = jnp.concatenate([pieces, remap_slot.astype(jnp.float32)[:, None]], axis=1)
    send_rows = jnp.full((slot_count, 257), -1.0, jnp.float32).at[position].set(tagged)
    got = lax.all_to_all(send_rows, ("sec", "tile"), split_axis=0, concat_axis=0, tiled=True)
    got_rows = got[:, :256]
    got_ids = got[:, 256].astype(jnp.int32)
    block_index = jnp.arange(block_count, dtype=jnp.int32)
    select = (got_ids[None, :] == block_index[:, None]).astype(jnp.float32)
    wave_blocks = jnp.dot(select, got_rows, precision=HIGHEST)
    wave_forcing = jnp.transpose(wave_blocks.reshape(block_count, 4, 64), (1, 0, 2)).reshape(
        4, node_count
    )
    alive_mask = live_nodes.astype(jnp.float32)[None, :]
    source_term, inflow = band_rates(
        wave_forcing, band_angle, band_speed, band_growth, facing_angle
    )
    energy = (wave_energy.astype(jnp.float32) + source_term) * alive_mask
    first_node = lax.axis_index(("sec", "tile")) * node_count
    total_rate = jnp.sum(inflow, axis=0)
    local_index = neighbors - first_node + 128
    sel = selection(local_index)
    wave_axis = ("sec", "tile")
    up = [(i, i + 1) for i in range(lax.axis_size(wave_axis) - 1)]
    down = [(j, i) for i, j in up]
    first, last = energy[:, :128], energy[:, -128:]
    for sweep in range(WSTEPS):
        left = lax.ppermute(last, wave_axis, up)
        right = lax.ppermute(first, wave_axis, down)
        energy, first, last = wave_sweep(left, energy, right, sel, inflow, total_rate, alive_mask)
    waves_out = energy.astype(jnp.bfloat16)
    coefficient = jnp.stack(
        [band_orbital * jnp.cos(band_angle), band_orbital * jnp.sin(band_angle)]
    )
    orbital = lax.psum(jnp.dot(coefficient, energy, precision=HIGHEST), "lev")
    orbital_blocks = jnp.transpose(orbital.reshape(2, block_count, 64), (1, 0, 2)).reshape(
        block_count, 128
    )
    back_rows = jnp.einsum("ws,wc->sc", select, orbital_blocks, precision=HIGHEST)
    returned = lax.all_to_all(back_rows, ("sec", "tile"), split_axis=0, concat_axis=0, tiled=True)
    mine = returned[position].reshape(entry_count, 2, 64)
    spread = jnp.einsum("eji,ecj->eci", weights, mine, precision=HIGHEST).reshape(entry_count, 128)
    ocean_select = (
        remap_cell[None, :] == jnp.arange(ocean_count, dtype=jnp.int32)[:, None]
    ).astype(jnp.float32)
    ocean_blocks = jnp.dot(ocean_select, spread, precision=HIGHEST)
    ocean_orbital = jnp.transpose(ocean_blocks.reshape(ocean_count, 2, 64), (1, 0, 2)).reshape(
        2, row_count, column_count
    )
    stress = TAU_CURRENT * current_square + TAU_WAVES * (
        ocean_orbital[0] * ocean_orbital[0] + ocean_orbital[1] * ocean_orbital[1]
    )
    erosion_gain = erosion_rate[:, None, None] * jnp.maximum(
        stress[None] / critical_stress[:, None, None] - 1.0, 0.0
    )
    classes = ocean_conc.shape[0]
    fields = jnp.concatenate(
        [
            ocean_conc,
            erosion_gain,
            jnp.stack(
                [
                    flow_lo.astype(jnp.float32),
                    flow_hi.astype(jnp.float32),
                    flow_y.astype(jnp.float32),
                    open_lo.astype(jnp.float32),
                    open_hi.astype(jnp.float32),
                    open_y.astype(jnp.float32),
                ]
            ),
        ]
    )
    wide = with_halo(fields, ((("sec", "tile"), 1),), OSTEPS)
    sediment = wide[:classes]
    gain = wide[classes : 2 * classes]
    lower_flow, upper_flow, side_flow, lower_open, upper_open, side_open = (
        wide[2 * classes + k] for k in range(6)
    )
    for sweep in range(OSTEPS):
        above_rows = jnp.pad(sediment, ((0, 0), (1, 0), (0, 0)))[:, :-1]
        below_rows = jnp.pad(sediment, ((0, 0), (0, 1), (0, 0)))[:, 1:]
        sediment = ocean_step(
            sediment,
            above_rows,
            below_rows,
            lower_flow,
            upper_flow,
            side_flow,
            lower_open,
            upper_open,
            side_open,
            settle_rate,
            gain,
        )
    sediment = sediment[:, OSTEPS : OSTEPS + row_count]
    return (sediment, waves_out)


def solution(mesh):
    return jax.shard_map(
        per_device,
        mesh=mesh,
        in_specs=(
            P("lev", ("sec", "tile"), None),
            P(("sec", "tile"), None),
            P(("sec", "tile"), None),
            P(("sec", "tile"), None),
            P(("sec", "tile"), None),
            P(("sec", "tile"), None),
            P(("sec", "tile"), None),
            P("lev"),
            P("lev"),
            P("lev"),
            P("lev", ("sec", "tile")),
            P("lev"),
            P("lev"),
            P("lev"),
            P("lev"),
            P(None, ("sec", "tile")),
            P(None, ("sec", "tile")),
            P(("sec", "tile")),
            P(("sec", "tile"), None),
            P(("sec", "tile")),
            P(("sec", "tile")),
            P(("sec", "tile"), None, None),
        ),
        out_specs=(P("lev", ("sec", "tile"), None), P("lev", ("sec", "tile"))),
        check_vma=False,
    )
```

```python
import jax
import jax.numpy as jnp
from jax import lax
from jax.experimental import pallas as pl
from jax.experimental.pallas import tpu as pltpu
from jax.sharding import PartitionSpec as P

OSTEPS = 4
WSTEPS = 4
NBRS = 4


KAPPA = 0.07
FORCE_SCALE = 5.0
DRAG = 50.0
TAU_CURRENT = 20.0
TAU_WAVES = 10.0
HIGHEST = lax.Precision.HIGHEST


def with_halo(x, sides, width):
    for axis, dim in sides:
        count, length = (lax.axis_size(axis), x.shape[dim])
        up = [(i, (i + 1) % count) for i in range(count - 1)]
        down = [(j, i) for i, j in up]
        last = lax.slice_in_dim(x, length - width, length, axis=dim)
        first = lax.slice_in_dim(x, 0, width, axis=dim)
        before = lax.ppermute(last, axis, up)
        after = lax.ppermute(first, axis, down)
        x = jnp.concatenate([before, x, after], axis=dim)
    return x


def coupling_fields(flow_lo, flow_hi, flow_y):
    eastward = 0.5 * (flow_lo.astype(jnp.float32) + flow_hi.astype(jnp.float32))
    across = flow_y.astype(jnp.float32)
    earlier = jnp.pad(across, ((0, 0), (1, 0)))[:, :-1]
    northward = 0.5 * (across + earlier)
    current_speed = jnp.sqrt(eastward * eastward + northward * northward)
    forcing = jnp.stack(
        [
            FORCE_SCALE * eastward,
            FORCE_SCALE * northward,
            DRAG * current_speed * eastward,
            DRAG * current_speed * northward,
        ]
    )
    return (forcing, eastward * eastward + northward * northward)


def band_rates(wave_forcing, band_dir, band_pace, growth, facing):
    cosines = jnp.cos(band_dir)[:, None]
    sine_terms = jnp.sin(band_dir)[:, None]
    drift_term = cosines * wave_forcing[0][None, :] + sine_terms * wave_forcing[1][None, :]
    push_term = jnp.maximum(
        cosines * wave_forcing[2][None, :] + sine_terms * wave_forcing[3][None, :], 0.0
    )
    base_rate = 0.5 * band_pace[:, None] * (1.0 + 0.5 * jnp.tanh(drift_term))
    facing_cos = jnp.cos(facing)[:, None, :]
    facing_sin = jnp.sin(facing)[:, None, :]
    along = cosines[None] * facing_cos + sine_terms[None] * facing_sin
    inflow = base_rate[None] * jnp.maximum(-along, 0.0)
    return (growth[:, None] * push_term, inflow)


def split2(x):
    hi = lax.reduce_precision(x, exponent_bits=8, mantissa_bits=7)
    return hi.astype(jnp.bfloat16), (x - hi).astype(jnp.bfloat16)


def sweep_kernel(
    left_ref, energy_ref, right_ref, sel_ref, inflow_ref, rate_ref, alive_ref, out_ref, first_ref, last_ref
):
    bands = out_ref.shape[0]
    tiles = sel_ref.shape[0]
    blocks = (
        [left_ref[...]]
        + [energy_ref[:, 128 * t : 128 * t + 128] for t in range(tiles)]
        + [right_ref[...]]
    )
    pieces = [split2(block) for block in blocks]
    for t in range(tiles):
        parts = jnp.concatenate(
            [jnp.concatenate([pieces[t + b][p] for b in range(3)], axis=1) for p in range(2)],
            axis=0,
        )
        picked = jnp.dot(parts, sel_ref[t], preferred_element_type=jnp.float32)
        gathered = picked[:bands] + picked[bands:]
        cols = slice(128 * t, 128 * t + 128)
        energy = blocks[t + 1]
        arriving = inflow_ref[0, :, cols] * gathered[:, 0:128]
        for k in range(1, NBRS):
            arriving = arriving + inflow_ref[k, :, cols] * gathered[:, 128 * k : 128 * k + 128]
        fresh = (energy + arriving - rate_ref[:, cols] * energy) * alive_ref[:, cols]
        out_ref[:, cols] = fresh
        if t == 0:
            first_ref[...] = fresh
        if t == tiles - 1:
            last_ref[...] = fresh


def wave_sweep(left, energy, right, sel, inflow, rate, alive):
    bands, nodes = rate.shape
    vmem = pl.BlockSpec(memory_space=pltpu.VMEM)
    flops = 2 * 2 * bands * 384 * nodes * NBRS
    moved = 4 * (2 * left.size + inflow.size + 3 * rate.size) + 2 * sel.size
    edge = jax.ShapeDtypeStruct((bands, 128), jnp.float32)
    return pl.pallas_call(
        sweep_kernel,
        out_shape=(jax.ShapeDtypeStruct((bands, nodes), jnp.float32), edge, edge),
        in_specs=[vmem] * 7,
        out_specs=(vmem, vmem, vmem),
        cost_estimate=pl.CostEstimate(flops=flops, bytes_accessed=moved, transcendentals=0),
    )(left, energy, right, sel, inflow, rate, alive)


def selection(local_index):
    nbrs, nodes = local_index.shape
    tiles = nodes // 128
    start = 128 * jnp.arange(tiles, dtype=jnp.int32)
    idx = local_index.reshape(nbrs, tiles, 128) - start[None, :, None]
    rows = jnp.arange(384, dtype=jnp.int32)
    sel = idx.transpose(1, 0, 2)[:, None, :, :] == rows[None, :, None, None]
    return sel.reshape(tiles, 384, nbrs * 128).astype(jnp.bfloat16)


def ocean_step(
    sediment,
    above_rows,
    below_rows,
    flow_lo,
    flow_hi,
    flow_y,
    open_lo,
    open_hi,
    open_y,
    settle_rate,
    erosion_gain,
):
    right_cells = jnp.pad(sediment, ((0, 0), (0, 0), (0, 1)))[:, :, 1:]
    flux_lo = (
        jnp.maximum(flow_lo, 0.0) * above_rows
        + jnp.minimum(flow_lo, 0.0) * sediment
        - KAPPA * open_lo * (sediment - above_rows)
    )
    flux_hi = (
        jnp.maximum(flow_hi, 0.0) * sediment
        + jnp.minimum(flow_hi, 0.0) * below_rows
        - KAPPA * open_hi * (below_rows - sediment)
    )
    flux_y = (
        jnp.maximum(flow_y, 0.0) * sediment
        + jnp.minimum(flow_y, 0.0) * right_cells
        - KAPPA * open_y * (right_cells - sediment)
    )
    flux_left = jnp.pad(flux_y, ((0, 0), (0, 0), (1, 0)))[:, :, :-1]
    return (
        sediment
        - (flux_hi - flux_lo)
        - (flux_y - flux_left)
        - settle_rate[:, None, None] * sediment
        + erosion_gain
    )


def entry_rank(owners, peer_count):
    onehot = (owners[:, None] == jnp.arange(peer_count, dtype=jnp.int32)[None, :]).astype(jnp.int32)
    earlier = jnp.cumsum(onehot, axis=0) - onehot
    return jnp.sum(earlier * onehot, axis=1)


def per_device(
    ocean_conc,
    flow_lo,
    flow_hi,
    flow_y,
    open_lo,
    open_hi,
    open_y,
    settle_rate,
    critical_stress,
    erosion_rate,
    wave_energy,
    band_angle,
    band_speed,
    band_growth,
    band_orbital,
    neighbors,
    facing_angle,
    live_nodes,
    remap_owner,
    remap_slot,
    remap_cell,
    remap_weight,
):
    peer_count = lax.axis_size(("sec", "tile"))
    entry_count = remap_cell.shape[0]
    capacity = min(entry_count, max(2, 2 * entry_count // peer_count))
    slot_count = peer_count * capacity
    row_count, column_count = flow_lo.shape
    ocean_count = row_count * column_count // 64
    node_count = wave_energy.shape[1]
    block_count = node_count // 64
    forcing, current_square = coupling_fields(flow_lo, flow_hi, flow_y)
    weights = remap_weight.astype(jnp.float32)
    picked = jnp.transpose(forcing.reshape(4, ocean_count, 64)[:, remap_cell, :], (1, 0, 2))
    pieces = jnp.einsum("eji,eci->ecj", weights, picked, precision=HIGHEST).reshape(
        entry_count, 256
    )
    owners = remap_owner[:, 0]
    ranking = entry_rank(owners, peer_count)
    position = owners * capacity + ranking
    tagged = jnp.concatenate([pieces, remap_slot.astype(jnp.float32)[:, None]], axis=1)
    send_rows = jnp.full((slot_count, 257), -1.0, jnp.float32).at[position].set(tagged)
    got = lax.all_to_all(send_rows, ("sec", "tile"), split_axis=0, concat_axis=0, tiled=True)
    got_rows = got[:, :256]
    got_ids = got[:, 256].astype(jnp.int32)
    block_index = jnp.arange(block_count, dtype=jnp.int32)
    select = (got_ids[None, :] == block_index[:, None]).astype(jnp.float32)
    wave_blocks = jnp.dot(select, got_rows, precision=HIGHEST)
    wave_forcing = jnp.transpose(wave_blocks.reshape(block_count, 4, 64), (1, 0, 2)).reshape(
        4, node_count
    )
    alive_mask = live_nodes.astype(jnp.float32)[None, :]
    source_term, inflow = band_rates(
        wave_forcing, band_angle, band_speed, band_growth, facing_angle
    )
    energy = (wave_energy.astype(jnp.float32) + source_term) * alive_mask
    first_node = lax.axis_index(("sec", "tile")) * node_count
    total_rate = jnp.sum(inflow, axis=0)
    local_index = neighbors - first_node + 128
    sel = selection(local_index)
    wave_axis = ("sec", "tile")
    up = [(i, i + 1) for i in range(lax.axis_size(wave_axis) - 1)]
    down = [(j, i) for i, j in up]
    first, last = energy[:, :128], energy[:, -128:]
    for sweep in range(WSTEPS):
        left = lax.ppermute(last, wave_axis, up)
        right = lax.ppermute(first, wave_axis, down)
        energy, first, last = wave_sweep(left, energy, right, sel, inflow, total_rate, alive_mask)
    waves_out = energy.astype(jnp.bfloat16)
    coefficient = jnp.stack(
        [band_orbital * jnp.cos(band_angle), band_orbital * jnp.sin(band_angle)]
    )
    orbital = lax.psum(jnp.dot(coefficient, energy, precision=HIGHEST), "lev")
    orbital_blocks = jnp.transpose(orbital.reshape(2, block_count, 64), (1, 0, 2)).reshape(
        block_count, 128
    )
    back_rows = jnp.einsum("ws,wc->sc", select, orbital_blocks, precision=HIGHEST)
    returned = lax.all_to_all(back_rows, ("sec", "tile"), split_axis=0, concat_axis=0, tiled=True)
    mine = returned[position].reshape(entry_count, 2, 64)
    spread = jnp.einsum("eji,ecj->eci", weights, mine, precision=HIGHEST).reshape(entry_count, 128)
    ocean_select = (
        remap_cell[None, :] == jnp.arange(ocean_count, dtype=jnp.int32)[:, None]
    ).astype(jnp.float32)
    ocean_blocks = jnp.dot(ocean_select, spread, precision=HIGHEST)
    ocean_orbital = jnp.transpose(ocean_blocks.reshape(ocean_count, 2, 64), (1, 0, 2)).reshape(
        2, row_count, column_count
    )
    stress = TAU_CURRENT * current_square + TAU_WAVES * (
        ocean_orbital[0] * ocean_orbital[0] + ocean_orbital[1] * ocean_orbital[1]
    )
    erosion_gain = erosion_rate[:, None, None] * jnp.maximum(
        stress[None] / critical_stress[:, None, None] - 1.0, 0.0
    )
    classes = ocean_conc.shape[0]
    fields = jnp.concatenate(
        [
            ocean_conc,
            erosion_gain,
            jnp.stack(
                [
                    flow_lo.astype(jnp.float32),
                    flow_hi.astype(jnp.float32),
                    flow_y.astype(jnp.float32),
                    open_lo.astype(jnp.float32),
                    open_hi.astype(jnp.float32),
                    open_y.astype(jnp.float32),
                ]
            ),
        ]
    )
    wide = with_halo(fields, ((("sec", "tile"), 1),), OSTEPS)
    sediment = wide[:classes]
    gain = wide[classes : 2 * classes]
    lower_flow, upper_flow, side_flow, lower_open, upper_open, side_open = (
        wide[2 * classes + k] for k in range(6)
    )
    for sweep in range(OSTEPS):
        above_rows = jnp.pad(sediment, ((0, 0), (1, 0), (0, 0)))[:, :-1]
        below_rows = jnp.pad(sediment, ((0, 0), (0, 1), (0, 0)))[:, 1:]
        sediment = ocean_step(
            sediment,
            above_rows,
            below_rows,
            lower_flow,
            upper_flow,
            side_flow,
            lower_open,
            upper_open,
            side_open,
            settle_rate,
            gain,
        )
    sediment = sediment[:, OSTEPS : OSTEPS + row_count]
    return (sediment, waves_out)


def solution(mesh):
    return jax.shard_map(
        per_device,
        mesh=mesh,
        in_specs=(
            P("lev", ("sec", "tile"), None),
            P(("sec", "tile"), None),
            P(("sec", "tile"), None),
            P(("sec", "tile"), None),
            P(("sec", "tile"), None),
            P(("sec", "tile"), None),
            P(("sec", "tile"), None),
            P("lev"),
            P("lev"),
            P("lev"),
            P("lev", ("sec", "tile")),
            P("lev"),
            P("lev"),
            P("lev"),
            P("lev"),
            P(None, ("sec", "tile")),
            P(None, ("sec", "tile")),
            P(("sec", "tile")),
            P(("sec", "tile"), None),
            P(("sec", "tile")),
            P(("sec", "tile")),
            P(("sec", "tile"), None, None),
        ),
        out_specs=(P("lev", ("sec", "tile"), None), P("lev", ("sec", "tile"))),
        check_vma=False,
    )
```

```python
import jax
import jax.numpy as jnp
from jax import lax
from jax.experimental import pallas as pl
from jax.experimental.pallas import tpu as pltpu
from jax.sharding import PartitionSpec as P

OSTEPS = 4
WSTEPS = 4
NBRS = 4


KAPPA = 0.07
FORCE_SCALE = 5.0
DRAG = 50.0
TAU_CURRENT = 20.0
TAU_WAVES = 10.0
HIGHEST = lax.Precision.HIGHEST


def with_halo(x, sides, width):
    for axis, dim in sides:
        count, length = (lax.axis_size(axis), x.shape[dim])
        up = [(i, (i + 1) % count) for i in range(count - 1)]
        down = [(j, i) for i, j in up]
        last = lax.slice_in_dim(x, length - width, length, axis=dim)
        first = lax.slice_in_dim(x, 0, width, axis=dim)
        before = lax.ppermute(last, axis, up)
        after = lax.ppermute(first, axis, down)
        x = jnp.concatenate([before, x, after], axis=dim)
    return x


def coupling_fields(flow_lo, flow_hi, flow_y):
    eastward = 0.5 * (flow_lo.astype(jnp.float32) + flow_hi.astype(jnp.float32))
    across = flow_y.astype(jnp.float32)
    earlier = jnp.pad(across, ((0, 0), (1, 0)))[:, :-1]
    northward = 0.5 * (across + earlier)
    current_speed = jnp.sqrt(eastward * eastward + northward * northward)
    forcing = jnp.stack(
        [
            FORCE_SCALE * eastward,
            FORCE_SCALE * northward,
            DRAG * current_speed * eastward,
            DRAG * current_speed * northward,
        ]
    )
    return (forcing, eastward * eastward + northward * northward)


def band_rates(wave_forcing, band_dir, band_pace, growth, facing):
    cosines = jnp.cos(band_dir)[:, None]
    sine_terms = jnp.sin(band_dir)[:, None]
    drift_term = cosines * wave_forcing[0][None, :] + sine_terms * wave_forcing[1][None, :]
    push_term = jnp.maximum(
        cosines * wave_forcing[2][None, :] + sine_terms * wave_forcing[3][None, :], 0.0
    )
    base_rate = 0.5 * band_pace[:, None] * (1.0 + 0.5 * jnp.tanh(drift_term))
    facing_cos = jnp.cos(facing)[:, None, :]
    facing_sin = jnp.sin(facing)[:, None, :]
    along = cosines[None] * facing_cos + sine_terms[None] * facing_sin
    inflow = base_rate[None] * jnp.maximum(-along, 0.0)
    return (growth[:, None] * push_term, inflow)


def split2(x):
    hi = lax.reduce_precision(x, exponent_bits=8, mantissa_bits=7)
    return hi.astype(jnp.bfloat16), (x - hi).astype(jnp.bfloat16)


def sweep_kernel(
    left_ref, energy_ref, right_ref, sel_ref, inflow_ref, rate_ref, alive_ref, out_ref, first_ref, last_ref
):
    bands = out_ref.shape[0]
    tiles = sel_ref.shape[0]
    blocks = (
        [left_ref[...]]
        + [energy_ref[:, 128 * t : 128 * t + 128] for t in range(tiles)]
        + [right_ref[...]]
    )
    pieces = [split2(block) for block in blocks]
    for t in range(tiles):
        parts = jnp.concatenate(
            [jnp.concatenate([pieces[t + b][p] for b in range(3)], axis=1) for p in range(2)],
            axis=0,
        )
        picked = jnp.dot(parts, sel_ref[t], preferred_element_type=jnp.float32)
        gathered = picked[:bands] + picked[bands:]
        cols = slice(128 * t, 128 * t + 128)
        energy = blocks[t + 1]
        arriving = inflow_ref[0, :, cols] * gathered[:, 0:128]
        for k in range(1, NBRS):
            arriving = arriving + inflow_ref[k, :, cols] * gathered[:, 128 * k : 128 * k + 128]
        fresh = (energy + arriving - rate_ref[:, cols] * energy) * alive_ref[:, cols]
        out_ref[:, cols] = fresh
        if t == 0:
            first_ref[...] = fresh
        if t == tiles - 1:
            last_ref[...] = fresh


def wave_sweep(left, energy, right, sel, inflow, rate, alive):
    bands, nodes = rate.shape
    vmem = pl.BlockSpec(memory_space=pltpu.VMEM)
    flops = 2 * 2 * bands * 384 * nodes * NBRS
    moved = 4 * (2 * left.size + inflow.size + 3 * rate.size) + 2 * sel.size
    edge = jax.ShapeDtypeStruct((bands, 128), jnp.float32)
    return pl.pallas_call(
        sweep_kernel,
        out_shape=(jax.ShapeDtypeStruct((bands, nodes), jnp.float32), edge, edge),
        in_specs=[vmem] * 7,
        out_specs=(vmem, vmem, vmem),
        cost_estimate=pl.CostEstimate(flops=flops, bytes_accessed=moved, transcendentals=0),
    )(left, energy, right, sel, inflow, rate, alive)


def selection(local_index):
    nbrs, nodes = local_index.shape
    tiles = nodes // 128
    start = 128 * jnp.arange(tiles, dtype=jnp.int32)
    idx = local_index.reshape(nbrs, tiles, 128) - start[None, :, None]
    rows = jnp.arange(384, dtype=jnp.int32)
    sel = idx.transpose(1, 0, 2)[:, None, :, :] == rows[None, :, None, None]
    return sel.reshape(tiles, 384, nbrs * 128).astype(jnp.bfloat16)


def ocean_step(
    sediment,
    above_rows,
    below_rows,
    flow_lo,
    flow_hi,
    flow_y,
    open_lo,
    open_hi,
    open_y,
    settle_rate,
    erosion_gain,
):
    right_cells = jnp.pad(sediment, ((0, 0), (0, 0), (0, 1)))[:, :, 1:]
    flux_lo = (
        jnp.maximum(flow_lo, 0.0) * above_rows
        + jnp.minimum(flow_lo, 0.0) * sediment
        - KAPPA * open_lo * (sediment - above_rows)
    )
    flux_hi = (
        jnp.maximum(flow_hi, 0.0) * sediment
        + jnp.minimum(flow_hi, 0.0) * below_rows
        - KAPPA * open_hi * (below_rows - sediment)
    )
    flux_y = (
        jnp.maximum(flow_y, 0.0) * sediment
        + jnp.minimum(flow_y, 0.0) * right_cells
        - KAPPA * open_y * (right_cells - sediment)
    )
    flux_left = jnp.pad(flux_y, ((0, 0), (0, 0), (1, 0)))[:, :, :-1]
    return (
        sediment
        - (flux_hi - flux_lo)
        - (flux_y - flux_left)
        - settle_rate[:, None, None] * sediment
        + erosion_gain
    )


def entry_rank(owners, peer_count):
    onehot = (owners[:, None] == jnp.arange(peer_count, dtype=jnp.int32)[None, :]).astype(jnp.int32)
    earlier = jnp.cumsum(onehot, axis=0) - onehot
    return jnp.sum(earlier * onehot, axis=1)


def per_device(
    ocean_conc,
    flow_lo,
    flow_hi,
    flow_y,
    open_lo,
    open_hi,
    open_y,
    settle_rate,
    critical_stress,
    erosion_rate,
    wave_energy,
    band_angle,
    band_speed,
    band_growth,
    band_orbital,
    neighbors,
    facing_angle,
    live_nodes,
    remap_owner,
    remap_slot,
    remap_cell,
    remap_weight,
):
    peer_count = lax.axis_size(("sec", "tile"))
    entry_count = remap_cell.shape[0]
    capacity = min(entry_count, max(2, 2 * entry_count // peer_count))
    slot_count = peer_count * capacity
    row_count, column_count = flow_lo.shape
    ocean_count = row_count * column_count // 64
    node_count = wave_energy.shape[1]
    block_count = node_count // 64
    forcing, current_square = coupling_fields(flow_lo, flow_hi, flow_y)
    weights = remap_weight.astype(jnp.float32)
    picked = jnp.transpose(forcing.reshape(4, ocean_count, 64)[:, remap_cell, :], (1, 0, 2))
    pieces = jnp.einsum("eji,eci->ecj", weights, picked, precision=HIGHEST).reshape(
        entry_count, 256
    )
    owners = remap_owner[:, 0]
    ranking = entry_rank(owners, peer_count)
    position = owners * capacity + ranking
    tagged = jnp.concatenate([pieces, remap_slot.astype(jnp.float32)[:, None]], axis=1)
    send_rows = jnp.full((slot_count, 257), -1.0, jnp.float32).at[position].set(tagged)
    packed = send_rows.reshape(peer_count, capacity * 257)
    got = lax.all_to_all(packed, ("sec", "tile"), split_axis=0, concat_axis=0, tiled=True)
    got = got.reshape(slot_count, 257)
    got_rows = got[:, :256]
    got_ids = got[:, 256].astype(jnp.int32)
    block_index = jnp.arange(block_count, dtype=jnp.int32)
    select = (got_ids[None, :] == block_index[:, None]).astype(jnp.float32)
    wave_blocks = jnp.dot(select, got_rows, precision=HIGHEST)
    wave_forcing = jnp.transpose(wave_blocks.reshape(block_count, 4, 64), (1, 0, 2)).reshape(
        4, node_count
    )
    alive_mask = live_nodes.astype(jnp.float32)[None, :]
    source_term, inflow = band_rates(
        wave_forcing, band_angle, band_speed, band_growth, facing_angle
    )
    energy = (wave_energy.astype(jnp.float32) + source_term) * alive_mask
    first_node = lax.axis_index(("sec", "tile")) * node_count
    total_rate = jnp.sum(inflow, axis=0)
    local_index = neighbors - first_node + 128
    sel = selection(local_index)
    wave_axis = ("sec", "tile")
    up = [(i, i + 1) for i in range(lax.axis_size(wave_axis) - 1)]
    down = [(j, i) for i, j in up]
    first, last = energy[:, :128], energy[:, -128:]
    for sweep in range(WSTEPS):
        left = lax.ppermute(last, wave_axis, up)
        right = lax.ppermute(first, wave_axis, down)
        energy, first, last = wave_sweep(left, energy, right, sel, inflow, total_rate, alive_mask)
    waves_out = energy.astype(jnp.bfloat16)
    coefficient = jnp.stack(
        [band_orbital * jnp.cos(band_angle), band_orbital * jnp.sin(band_angle)]
    )
    orbital = lax.psum(jnp.dot(coefficient, energy, precision=HIGHEST), "lev")
    orbital_blocks = jnp.transpose(orbital.reshape(2, block_count, 64), (1, 0, 2)).reshape(
        block_count, 128
    )
    back_rows = jnp.einsum("ws,wc->sc", select, orbital_blocks, precision=HIGHEST)
    returned = lax.all_to_all(back_rows, ("sec", "tile"), split_axis=0, concat_axis=0, tiled=True)
    mine = returned[position].reshape(entry_count, 2, 64)
    spread = jnp.einsum("eji,ecj->eci", weights, mine, precision=HIGHEST).reshape(entry_count, 128)
    ocean_select = (
        remap_cell[None, :] == jnp.arange(ocean_count, dtype=jnp.int32)[:, None]
    ).astype(jnp.float32)
    ocean_blocks = jnp.dot(ocean_select, spread, precision=HIGHEST)
    ocean_orbital = jnp.transpose(ocean_blocks.reshape(ocean_count, 2, 64), (1, 0, 2)).reshape(
        2, row_count, column_count
    )
    stress = TAU_CURRENT * current_square + TAU_WAVES * (
        ocean_orbital[0] * ocean_orbital[0] + ocean_orbital[1] * ocean_orbital[1]
    )
    erosion_gain = erosion_rate[:, None, None] * jnp.maximum(
        stress[None] / critical_stress[:, None, None] - 1.0, 0.0
    )
    classes = ocean_conc.shape[0]
    fields = jnp.concatenate(
        [
            ocean_conc,
            erosion_gain,
            jnp.stack(
                [
                    flow_lo.astype(jnp.float32),
                    flow_hi.astype(jnp.float32),
                    flow_y.astype(jnp.float32),
                    open_lo.astype(jnp.float32),
                    open_hi.astype(jnp.float32),
                    open_y.astype(jnp.float32),
                ]
            ),
        ]
    )
    wide = with_halo(fields, ((("sec", "tile"), 1),), OSTEPS)
    sediment = wide[:classes]
    gain = wide[classes : 2 * classes]
    lower_flow, upper_flow, side_flow, lower_open, upper_open, side_open = (
        wide[2 * classes + k] for k in range(6)
    )
    for sweep in range(OSTEPS):
        above_rows = jnp.pad(sediment, ((0, 0), (1, 0), (0, 0)))[:, :-1]
        below_rows = jnp.pad(sediment, ((0, 0), (0, 1), (0, 0)))[:, 1:]
        sediment = ocean_step(
            sediment,
            above_rows,
            below_rows,
            lower_flow,
            upper_flow,
            side_flow,
            lower_open,
            upper_open,
            side_open,
            settle_rate,
            gain,
        )
    sediment = sediment[:, OSTEPS : OSTEPS + row_count]
    return (sediment, waves_out)


def solution(mesh):
    return jax.shard_map(
        per_device,
        mesh=mesh,
        in_specs=(
            P("lev", ("sec", "tile"), None),
            P(("sec", "tile"), None),
            P(("sec", "tile"), None),
            P(("sec", "tile"), None),
            P(("sec", "tile"), None),
            P(("sec", "tile"), None),
            P(("sec", "tile"), None),
            P("lev"),
            P("lev"),
            P("lev"),
            P("lev", ("sec", "tile")),
            P("lev"),
            P("lev"),
            P("lev"),
            P("lev"),
            P(None, ("sec", "tile")),
            P(None, ("sec", "tile")),
            P(("sec", "tile")),
            P(("sec", "tile"), None),
            P(("sec", "tile")),
            P(("sec", "tile")),
            P(("sec", "tile"), None, None),
        ),
        out_specs=(P("lev", ("sec", "tile"), None), P("lev", ("sec", "tile"))),
        check_vma=False,
    )
```

```python
import functools

import jax
import jax.numpy as jnp
from jax import lax
from jax.experimental import pallas as pl
from jax.experimental.pallas import tpu as pltpu
from jax.sharding import PartitionSpec as P

OSTEPS = 4
WSTEPS = 4
NBRS = 4


KAPPA = 0.07
FORCE_SCALE = 5.0
DRAG = 50.0
TAU_CURRENT = 20.0
TAU_WAVES = 10.0
HIGHEST = lax.Precision.HIGHEST


def with_halo(x, sides, width):
    for axis, dim in sides:
        count, length = (lax.axis_size(axis), x.shape[dim])
        up = [(i, (i + 1) % count) for i in range(count - 1)]
        down = [(j, i) for i, j in up]
        last = lax.slice_in_dim(x, length - width, length, axis=dim)
        first = lax.slice_in_dim(x, 0, width, axis=dim)
        before = lax.ppermute(last, axis, up)
        after = lax.ppermute(first, axis, down)
        x = jnp.concatenate([before, x, after], axis=dim)
    return x


def coupling_fields(flow_lo, flow_hi, flow_y):
    eastward = 0.5 * (flow_lo.astype(jnp.float32) + flow_hi.astype(jnp.float32))
    across = flow_y.astype(jnp.float32)
    earlier = jnp.pad(across, ((0, 0), (1, 0)))[:, :-1]
    northward = 0.5 * (across + earlier)
    current_speed = jnp.sqrt(eastward * eastward + northward * northward)
    forcing = jnp.stack(
        [
            FORCE_SCALE * eastward,
            FORCE_SCALE * northward,
            DRAG * current_speed * eastward,
            DRAG * current_speed * northward,
        ]
    )
    return (forcing, eastward * eastward + northward * northward)


def band_rates(wave_forcing, band_dir, band_pace, growth, facing):
    cosines = jnp.cos(band_dir)[:, None]
    sine_terms = jnp.sin(band_dir)[:, None]
    drift_term = cosines * wave_forcing[0][None, :] + sine_terms * wave_forcing[1][None, :]
    push_term = jnp.maximum(
        cosines * wave_forcing[2][None, :] + sine_terms * wave_forcing[3][None, :], 0.0
    )
    base_rate = 0.5 * band_pace[:, None] * (1.0 + 0.5 * jnp.tanh(drift_term))
    facing_cos = jnp.cos(facing)[:, None, :]
    facing_sin = jnp.sin(facing)[:, None, :]
    along = cosines[None] * facing_cos + sine_terms[None] * facing_sin
    inflow = base_rate[None] * jnp.maximum(-along, 0.0)
    return (growth[:, None] * push_term, inflow)


def split2(x):
    hi = lax.reduce_precision(x, exponent_bits=8, mantissa_bits=7)
    return hi.astype(jnp.bfloat16), (x - hi).astype(jnp.bfloat16)


def tile_kernel(count, *refs):
    blocks = [ref[...] for ref in refs[: 3 * count]]
    sel_refs = refs[3 * count : 4 * count]
    inflow_refs = refs[4 * count : 5 * count]
    rate_refs = refs[5 * count : 6 * count]
    alive_refs = refs[6 * count : 7 * count]
    out_refs = refs[7 * count :]
    bands = blocks[0].shape[0]
    pieces = [split2(block) for block in blocks]
    for i in range(count):
        parts = jnp.concatenate(
            [jnp.concatenate([pieces[3 * i + b][p] for b in range(3)], axis=1) for p in range(2)],
            axis=0,
        )
        picked = jnp.dot(parts, sel_refs[i][...], preferred_element_type=jnp.float32)
        gathered = picked[:bands] + picked[bands:]
        energy = blocks[3 * i + 1]
        arriving = inflow_refs[i][0] * gathered[:, 0:128]
        for k in range(1, NBRS):
            arriving = arriving + inflow_refs[i][k] * gathered[:, 128 * k : 128 * k + 128]
        out_refs[i][...] = (energy + arriving - rate_refs[i][...] * energy) * alive_refs[i][...]


def sweep_tiles(windows, sels, inflows, rates, alives):
    count = len(sels)
    bands = windows[0].shape[0]
    vmem = pl.BlockSpec(memory_space=pltpu.VMEM)
    operands = list(windows) + list(sels) + list(inflows) + list(rates) + list(alives)
    flops = 2 * 2 * bands * 384 * 128 * NBRS * count
    moved = sum(4 * x.size for x in windows + inflows + rates) + sum(2 * x.size for x in sels)
    edge = jax.ShapeDtypeStruct((bands, 128), jnp.float32)
    return pl.pallas_call(
        functools.partial(tile_kernel, count),
        out_shape=tuple([edge] * count),
        in_specs=[vmem] * len(operands),
        out_specs=tuple([vmem] * count),
        cost_estimate=pl.CostEstimate(flops=flops, bytes_accessed=moved, transcendentals=0),
    )(*operands)


def selection(local_index):
    nbrs, nodes = local_index.shape
    tiles = nodes // 128
    start = 128 * jnp.arange(tiles, dtype=jnp.int32)
    idx = local_index.reshape(nbrs, tiles, 128) - start[None, :, None]
    rows = jnp.arange(384, dtype=jnp.int32)
    sel = idx.transpose(1, 0, 2)[:, None, :, :] == rows[None, :, None, None]
    return sel.reshape(tiles, 384, nbrs * 128).astype(jnp.bfloat16)


def ocean_step(
    sediment,
    above_rows,
    below_rows,
    flow_lo,
    flow_hi,
    flow_y,
    open_lo,
    open_hi,
    open_y,
    settle_rate,
    erosion_gain,
):
    right_cells = jnp.pad(sediment, ((0, 0), (0, 0), (0, 1)))[:, :, 1:]
    flux_lo = (
        jnp.maximum(flow_lo, 0.0) * above_rows
        + jnp.minimum(flow_lo, 0.0) * sediment
        - KAPPA * open_lo * (sediment - above_rows)
    )
    flux_hi = (
        jnp.maximum(flow_hi, 0.0) * sediment
        + jnp.minimum(flow_hi, 0.0) * below_rows
        - KAPPA * open_hi * (below_rows - sediment)
    )
    flux_y = (
        jnp.maximum(flow_y, 0.0) * sediment
        + jnp.minimum(flow_y, 0.0) * right_cells
        - KAPPA * open_y * (right_cells - sediment)
    )
    flux_left = jnp.pad(flux_y, ((0, 0), (0, 0), (1, 0)))[:, :, :-1]
    return (
        sediment
        - (flux_hi - flux_lo)
        - (flux_y - flux_left)
        - settle_rate[:, None, None] * sediment
        + erosion_gain
    )


def entry_rank(owners, peer_count):
    onehot = (owners[:, None] == jnp.arange(peer_count, dtype=jnp.int32)[None, :]).astype(jnp.int32)
    earlier = jnp.cumsum(onehot, axis=0) - onehot
    return jnp.sum(earlier * onehot, axis=1)


def per_device(
    ocean_conc,
    flow_lo,
    flow_hi,
    flow_y,
    open_lo,
    open_hi,
    open_y,
    settle_rate,
    critical_stress,
    erosion_rate,
    wave_energy,
    band_angle,
    band_speed,
    band_growth,
    band_orbital,
    neighbors,
    facing_angle,
    live_nodes,
    remap_owner,
    remap_slot,
    remap_cell,
    remap_weight,
):
    peer_count = lax.axis_size(("sec", "tile"))
    entry_count = remap_cell.shape[0]
    capacity = min(entry_count, max(2, 2 * entry_count // peer_count))
    slot_count = peer_count * capacity
    row_count, column_count = flow_lo.shape
    ocean_count = row_count * column_count // 64
    node_count = wave_energy.shape[1]
    block_count = node_count // 64
    forcing, current_square = coupling_fields(flow_lo, flow_hi, flow_y)
    weights = remap_weight.astype(jnp.float32)
    picked = jnp.transpose(forcing.reshape(4, ocean_count, 64)[:, remap_cell, :], (1, 0, 2))
    pieces = jnp.einsum("eji,eci->ecj", weights, picked, precision=HIGHEST).reshape(
        entry_count, 256
    )
    owners = remap_owner[:, 0]
    ranking = entry_rank(owners, peer_count)
    position = owners * capacity + ranking
    tagged = jnp.concatenate([pieces, remap_slot.astype(jnp.float32)[:, None]], axis=1)
    send_rows = jnp.full((slot_count, 257), -1.0, jnp.float32).at[position].set(tagged)
    packed = send_rows.reshape(peer_count, capacity * 257)
    got = lax.all_to_all(packed, ("sec", "tile"), split_axis=0, concat_axis=0, tiled=True)
    got = got.reshape(slot_count, 257)
    got_rows = got[:, :256]
    got_ids = got[:, 256].astype(jnp.int32)
    block_index = jnp.arange(block_count, dtype=jnp.int32)
    select = (got_ids[None, :] == block_index[:, None]).astype(jnp.float32)
    wave_blocks = jnp.dot(select, got_rows, precision=HIGHEST)
    wave_forcing = jnp.transpose(wave_blocks.reshape(block_count, 4, 64), (1, 0, 2)).reshape(
        4, node_count
    )
    alive_mask = live_nodes.astype(jnp.float32)[None, :]
    source_term, inflow = band_rates(
        wave_forcing, band_angle, band_speed, band_growth, facing_angle
    )
    energy = (wave_energy.astype(jnp.float32) + source_term) * alive_mask
    first_node = lax.axis_index(("sec", "tile")) * node_count
    total_rate = jnp.sum(inflow, axis=0)
    local_index = neighbors - first_node + 128
    sel = selection(local_index)
    wave_axis = ("sec", "tile")
    up = [(i, i + 1) for i in range(lax.axis_size(wave_axis) - 1)]
    down = [(j, i) for i, j in up]
    tiles = node_count // 128
    cut = lambda x, t: x[..., 128 * t : 128 * t + 128]
    sels = [sel[t] for t in range(tiles)]
    inflows = [cut(inflow, t) for t in range(tiles)]
    rates = [cut(total_rate, t) for t in range(tiles)]
    alives = [cut(alive_mask, t) for t in range(tiles)]
    blocks = [cut(energy, t) for t in range(tiles)]
    inner = list(range(1, tiles - 1))
    for sweep in range(WSTEPS):
        left = lax.ppermute(blocks[-1], wave_axis, up)
        right = lax.ppermute(blocks[0], wave_axis, down)
        middle = sweep_tiles(
            [block for t in inner for block in blocks[t - 1 : t + 2]],
            [sels[t] for t in inner],
            [inflows[t] for t in inner],
            [rates[t] for t in inner],
            [alives[t] for t in inner],
        )
        ends = (0, tiles - 1)
        first, last = sweep_tiles(
            [left] + blocks[:2] + blocks[-2:] + [right],
            [sels[t] for t in ends],
            [inflows[t] for t in ends],
            [rates[t] for t in ends],
            [alives[t] for t in ends],
        )
        blocks = [first] + list(middle) + [last]
    energy = jnp.concatenate(blocks, axis=1)
    waves_out = energy.astype(jnp.bfloat16)
    coefficient = jnp.stack(
        [band_orbital * jnp.cos(band_angle), band_orbital * jnp.sin(band_angle)]
    )
    orbital = lax.psum(jnp.dot(coefficient, energy, precision=HIGHEST), "lev")
    orbital_blocks = jnp.transpose(orbital.reshape(2, block_count, 64), (1, 0, 2)).reshape(
        block_count, 128
    )
    back_rows = jnp.einsum("ws,wc->sc", select, orbital_blocks, precision=HIGHEST)
    returned = lax.all_to_all(back_rows, ("sec", "tile"), split_axis=0, concat_axis=0, tiled=True)
    mine = returned[position].reshape(entry_count, 2, 64)
    spread = jnp.einsum("eji,ecj->eci", weights, mine, precision=HIGHEST).reshape(entry_count, 128)
    ocean_select = (
        remap_cell[None, :] == jnp.arange(ocean_count, dtype=jnp.int32)[:, None]
    ).astype(jnp.float32)
    ocean_blocks = jnp.dot(ocean_select, spread, precision=HIGHEST)
    ocean_orbital = jnp.transpose(ocean_blocks.reshape(ocean_count, 2, 64), (1, 0, 2)).reshape(
        2, row_count, column_count
    )
    stress = TAU_CURRENT * current_square + TAU_WAVES * (
        ocean_orbital[0] * ocean_orbital[0] + ocean_orbital[1] * ocean_orbital[1]
    )
    erosion_gain = erosion_rate[:, None, None] * jnp.maximum(
        stress[None] / critical_stress[:, None, None] - 1.0, 0.0
    )
    classes = ocean_conc.shape[0]
    fields = jnp.concatenate(
        [
            ocean_conc,
            erosion_gain,
            jnp.stack(
                [
                    flow_lo.astype(jnp.float32),
                    flow_hi.astype(jnp.float32),
                    flow_y.astype(jnp.float32),
                    open_lo.astype(jnp.float32),
                    open_hi.astype(jnp.float32),
                    open_y.astype(jnp.float32),
                ]
            ),
        ]
    )
    wide = with_halo(fields, ((("sec", "tile"), 1),), OSTEPS)
    sediment = wide[:classes]
    gain = wide[classes : 2 * classes]
    lower_flow, upper_flow, side_flow, lower_open, upper_open, side_open = (
        wide[2 * classes + k] for k in range(6)
    )
    for sweep in range(OSTEPS):
        above_rows = jnp.pad(sediment, ((0, 0), (1, 0), (0, 0)))[:, :-1]
        below_rows = jnp.pad(sediment, ((0, 0), (0, 1), (0, 0)))[:, 1:]
        sediment = ocean_step(
            sediment,
            above_rows,
            below_rows,
            lower_flow,
            upper_flow,
            side_flow,
            lower_open,
            upper_open,
            side_open,
            settle_rate,
            gain,
        )
    sediment = sediment[:, OSTEPS : OSTEPS + row_count]
    return (sediment, waves_out)


def solution(mesh):
    return jax.shard_map(
        per_device,
        mesh=mesh,
        in_specs=(
            P("lev", ("sec", "tile"), None),
            P(("sec", "tile"), None),
            P(("sec", "tile"), None),
            P(("sec", "tile"), None),
            P(("sec", "tile"), None),
            P(("sec", "tile"), None),
            P(("sec", "tile"), None),
            P("lev"),
            P("lev"),
            P("lev"),
            P("lev", ("sec", "tile")),
            P("lev"),
            P("lev"),
            P("lev"),
            P("lev"),
            P(None, ("sec", "tile")),
            P(None, ("sec", "tile")),
            P(("sec", "tile")),
            P(("sec", "tile"), None),
            P(("sec", "tile")),
            P(("sec", "tile")),
            P(("sec", "tile"), None, None),
        ),
        out_specs=(P("lev", ("sec", "tile"), None), P("lev", ("sec", "tile"))),
        check_vma=False,
    )
```

```python
import jax
import jax.numpy as jnp
from jax import lax
from jax.experimental import pallas as pl
from jax.experimental.pallas import tpu as pltpu
from jax.sharding import PartitionSpec as P

OSTEPS = 4
WSTEPS = 4
NBRS = 4


KAPPA = 0.07
FORCE_SCALE = 5.0
DRAG = 50.0
TAU_CURRENT = 20.0
TAU_WAVES = 10.0
HIGHEST = lax.Precision.HIGHEST


def with_halo(x, sides, width):
    for axis, dim in sides:
        count, length = (lax.axis_size(axis), x.shape[dim])
        up = [(i, (i + 1) % count) for i in range(count - 1)]
        down = [(j, i) for i, j in up]
        last = lax.slice_in_dim(x, length - width, length, axis=dim)
        first = lax.slice_in_dim(x, 0, width, axis=dim)
        before = lax.ppermute(last, axis, up)
        after = lax.ppermute(first, axis, down)
        x = jnp.concatenate([before, x, after], axis=dim)
    return x


def coupling_fields(flow_lo, flow_hi, flow_y):
    eastward = 0.5 * (flow_lo.astype(jnp.float32) + flow_hi.astype(jnp.float32))
    across = flow_y.astype(jnp.float32)
    earlier = jnp.pad(across, ((0, 0), (1, 0)))[:, :-1]
    northward = 0.5 * (across + earlier)
    current_speed = jnp.sqrt(eastward * eastward + northward * northward)
    forcing = jnp.stack(
        [
            FORCE_SCALE * eastward,
            FORCE_SCALE * northward,
            DRAG * current_speed * eastward,
            DRAG * current_speed * northward,
        ]
    )
    return (forcing, eastward * eastward + northward * northward)


def band_rates(wave_forcing, band_dir, band_pace, growth, facing):
    cosines = jnp.cos(band_dir)[:, None]
    sine_terms = jnp.sin(band_dir)[:, None]
    drift_term = cosines * wave_forcing[0][None, :] + sine_terms * wave_forcing[1][None, :]
    push_term = jnp.maximum(
        cosines * wave_forcing[2][None, :] + sine_terms * wave_forcing[3][None, :], 0.0
    )
    base_rate = 0.5 * band_pace[:, None] * (1.0 + 0.5 * jnp.tanh(drift_term))
    facing_cos = jnp.cos(facing)[:, None, :]
    facing_sin = jnp.sin(facing)[:, None, :]
    along = cosines[None] * facing_cos + sine_terms[None] * facing_sin
    inflow = base_rate[None] * jnp.maximum(-along, 0.0)
    return (growth[:, None] * push_term, inflow)


def split2(x):
    hi = lax.reduce_precision(x, exponent_bits=8, mantissa_bits=7)
    return hi.astype(jnp.bfloat16), (x - hi).astype(jnp.bfloat16)


def sweep_kernel(
    left_ref,
    energy_ref,
    right_ref,
    sel_hbm,
    inflow_hbm,
    rate_ref,
    alive_ref,
    out_ref,
    first_ref,
    last_ref,
    sel_ref,
    inflow_ref,
    sems,
):
    bands = out_ref.shape[0]
    tiles = sel_ref.shape[0]
    copies = []
    for t in range(tiles):
        span = pl.ds(128 * t, 128)
        pair = (
            pltpu.make_async_copy(sel_hbm.at[t], sel_ref.at[t], sems.at[0, t]),
            pltpu.make_async_copy(inflow_hbm.at[:, :, span], inflow_ref.at[:, :, span], sems.at[1, t]),
        )
        pair[0].start()
        pair[1].start()
        copies.append(pair)
    blocks = (
        [left_ref[...]]
        + [energy_ref[:, 128 * t : 128 * t + 128] for t in range(tiles)]
        + [right_ref[...]]
    )
    pieces = [split2(block) for block in blocks]
    for t in range(tiles):
        parts = jnp.concatenate(
            [jnp.concatenate([pieces[t + b][p] for b in range(3)], axis=1) for p in range(2)],
            axis=0,
        )
        copies[t][0].wait()
        picked = jnp.dot(parts, sel_ref[t], preferred_element_type=jnp.float32)
        copies[t][1].wait()
        gathered = picked[:bands] + picked[bands:]
        cols = slice(128 * t, 128 * t + 128)
        energy = blocks[t + 1]
        arriving = inflow_ref[0, :, cols] * gathered[:, 0:128]
        for k in range(1, NBRS):
            arriving = arriving + inflow_ref[k, :, cols] * gathered[:, 128 * k : 128 * k + 128]
        fresh = (energy + arriving - rate_ref[:, cols] * energy) * alive_ref[:, cols]
        out_ref[:, cols] = fresh
        if t == 0:
            first_ref[...] = fresh
        if t == tiles - 1:
            last_ref[...] = fresh


def wave_sweep(left, energy, right, sel, inflow, rate, alive):
    bands, nodes = rate.shape
    vmem = pl.BlockSpec(memory_space=pltpu.VMEM)
    flops = 2 * 2 * bands * 384 * nodes * NBRS
    moved = 4 * (2 * left.size + inflow.size + 3 * rate.size) + 2 * sel.size
    edge = jax.ShapeDtypeStruct((bands, 128), jnp.float32)
    return pl.pallas_call(
        sweep_kernel,
        out_shape=(jax.ShapeDtypeStruct((bands, nodes), jnp.float32), edge, edge),
        in_specs=[vmem] * 3 + [pl.BlockSpec(memory_space=pl.ANY)] * 2 + [vmem] * 2,
        out_specs=(vmem, vmem, vmem),
        scratch_shapes=[
            pltpu.VMEM(sel.shape, sel.dtype),
            pltpu.VMEM(inflow.shape, inflow.dtype),
            pltpu.SemaphoreType.DMA((2, sel.shape[0])),
        ],
        cost_estimate=pl.CostEstimate(flops=flops, bytes_accessed=moved, transcendentals=0),
    )(left, energy, right, sel, inflow, rate, alive)


def selection(local_index):
    nbrs, nodes = local_index.shape
    tiles = nodes // 128
    start = 128 * jnp.arange(tiles, dtype=jnp.int32)
    idx = local_index.reshape(nbrs, tiles, 128) - start[None, :, None]
    rows = jnp.arange(384, dtype=jnp.int32)
    sel = idx.transpose(1, 0, 2)[:, None, :, :] == rows[None, :, None, None]
    return sel.reshape(tiles, 384, nbrs * 128).astype(jnp.bfloat16)


def ocean_step(
    sediment,
    above_rows,
    below_rows,
    flow_lo,
    flow_hi,
    flow_y,
    open_lo,
    open_hi,
    open_y,
    settle_rate,
    erosion_gain,
):
    right_cells = jnp.pad(sediment, ((0, 0), (0, 0), (0, 1)))[:, :, 1:]
    flux_lo = (
        jnp.maximum(flow_lo, 0.0) * above_rows
        + jnp.minimum(flow_lo, 0.0) * sediment
        - KAPPA * open_lo * (sediment - above_rows)
    )
    flux_hi = (
        jnp.maximum(flow_hi, 0.0) * sediment
        + jnp.minimum(flow_hi, 0.0) * below_rows
        - KAPPA * open_hi * (below_rows - sediment)
    )
    flux_y = (
        jnp.maximum(flow_y, 0.0) * sediment
        + jnp.minimum(flow_y, 0.0) * right_cells
        - KAPPA * open_y * (right_cells - sediment)
    )
    flux_left = jnp.pad(flux_y, ((0, 0), (0, 0), (1, 0)))[:, :, :-1]
    return (
        sediment
        - (flux_hi - flux_lo)
        - (flux_y - flux_left)
        - settle_rate[:, None, None] * sediment
        + erosion_gain
    )


def entry_rank(owners, peer_count):
    onehot = (owners[:, None] == jnp.arange(peer_count, dtype=jnp.int32)[None, :]).astype(jnp.int32)
    earlier = jnp.cumsum(onehot, axis=0) - onehot
    return jnp.sum(earlier * onehot, axis=1)


def per_device(
    ocean_conc,
    flow_lo,
    flow_hi,
    flow_y,
    open_lo,
    open_hi,
    open_y,
    settle_rate,
    critical_stress,
    erosion_rate,
    wave_energy,
    band_angle,
    band_speed,
    band_growth,
    band_orbital,
    neighbors,
    facing_angle,
    live_nodes,
    remap_owner,
    remap_slot,
    remap_cell,
    remap_weight,
):
    peer_count = lax.axis_size(("sec", "tile"))
    entry_count = remap_cell.shape[0]
    capacity = min(entry_count, max(2, 2 * entry_count // peer_count))
    slot_count = peer_count * capacity
    row_count, column_count = flow_lo.shape
    ocean_count = row_count * column_count // 64
    node_count = wave_energy.shape[1]
    block_count = node_count // 64
    forcing, current_square = coupling_fields(flow_lo, flow_hi, flow_y)
    weights = remap_weight.astype(jnp.float32)
    picked = jnp.transpose(forcing.reshape(4, ocean_count, 64)[:, remap_cell, :], (1, 0, 2))
    pieces = jnp.einsum("eji,eci->ecj", weights, picked, precision=HIGHEST).reshape(
        entry_count, 256
    )
    owners = remap_owner[:, 0]
    ranking = entry_rank(owners, peer_count)
    position = owners * capacity + ranking
    tagged = jnp.concatenate([pieces, remap_slot.astype(jnp.float32)[:, None]], axis=1)
    send_rows = jnp.full((slot_count, 257), -1.0, jnp.float32).at[position].set(tagged)
    packed = send_rows.reshape(peer_count, capacity * 257)
    got = lax.all_to_all(packed, ("sec", "tile"), split_axis=0, concat_axis=0, tiled=True)
    got = got.reshape(slot_count, 257)
    got_rows = got[:, :256]
    got_ids = got[:, 256].astype(jnp.int32)
    block_index = jnp.arange(block_count, dtype=jnp.int32)
    select = (got_ids[None, :] == block_index[:, None]).astype(jnp.float32)
    wave_blocks = jnp.dot(select, got_rows, precision=HIGHEST)
    wave_forcing = jnp.transpose(wave_blocks.reshape(block_count, 4, 64), (1, 0, 2)).reshape(
        4, node_count
    )
    alive_mask = live_nodes.astype(jnp.float32)[None, :]
    source_term, inflow = band_rates(
        wave_forcing, band_angle, band_speed, band_growth, facing_angle
    )
    energy = (wave_energy.astype(jnp.float32) + source_term) * alive_mask
    first_node = lax.axis_index(("sec", "tile")) * node_count
    total_rate = jnp.sum(inflow, axis=0)
    local_index = neighbors - first_node + 128
    sel = selection(local_index)
    wave_axis = ("sec", "tile")
    up = [(i, i + 1) for i in range(lax.axis_size(wave_axis) - 1)]
    down = [(j, i) for i, j in up]
    first, last = energy[:, :128], energy[:, -128:]
    for sweep in range(WSTEPS):
        left = lax.ppermute(last, wave_axis, up)
        right = lax.ppermute(first, wave_axis, down)
        energy, first, last = wave_sweep(left, energy, right, sel, inflow, total_rate, alive_mask)
    waves_out = energy.astype(jnp.bfloat16)
    coefficient = jnp.stack(
        [band_orbital * jnp.cos(band_angle), band_orbital * jnp.sin(band_angle)]
    )
    orbital = lax.psum(jnp.dot(coefficient, energy, precision=HIGHEST), "lev")
    orbital_blocks = jnp.transpose(orbital.reshape(2, block_count, 64), (1, 0, 2)).reshape(
        block_count, 128
    )
    back_rows = jnp.einsum("ws,wc->sc", select, orbital_blocks, precision=HIGHEST)
    returned = lax.all_to_all(back_rows, ("sec", "tile"), split_axis=0, concat_axis=0, tiled=True)
    mine = returned[position].reshape(entry_count, 2, 64)
    spread = jnp.einsum("eji,ecj->eci", weights, mine, precision=HIGHEST).reshape(entry_count, 128)
    ocean_select = (
        remap_cell[None, :] == jnp.arange(ocean_count, dtype=jnp.int32)[:, None]
    ).astype(jnp.float32)
    ocean_blocks = jnp.dot(ocean_select, spread, precision=HIGHEST)
    ocean_orbital = jnp.transpose(ocean_blocks.reshape(ocean_count, 2, 64), (1, 0, 2)).reshape(
        2, row_count, column_count
    )
    stress = TAU_CURRENT * current_square + TAU_WAVES * (
        ocean_orbital[0] * ocean_orbital[0] + ocean_orbital[1] * ocean_orbital[1]
    )
    erosion_gain = erosion_rate[:, None, None] * jnp.maximum(
        stress[None] / critical_stress[:, None, None] - 1.0, 0.0
    )
    classes = ocean_conc.shape[0]
    fields = jnp.concatenate(
        [
            ocean_conc,
            erosion_gain,
            jnp.stack(
                [
                    flow_lo.astype(jnp.float32),
                    flow_hi.astype(jnp.float32),
                    flow_y.astype(jnp.float32),
                    open_lo.astype(jnp.float32),
                    open_hi.astype(jnp.float32),
                    open_y.astype(jnp.float32),
                ]
            ),
        ]
    )
    wide = with_halo(fields, ((("sec", "tile"), 1),), OSTEPS)
    sediment = wide[:classes]
    gain = wide[classes : 2 * classes]
    lower_flow, upper_flow, side_flow, lower_open, upper_open, side_open = (
        wide[2 * classes + k] for k in range(6)
    )
    for sweep in range(OSTEPS):
        above_rows = jnp.pad(sediment, ((0, 0), (1, 0), (0, 0)))[:, :-1]
        below_rows = jnp.pad(sediment, ((0, 0), (0, 1), (0, 0)))[:, 1:]
        sediment = ocean_step(
            sediment,
            above_rows,
            below_rows,
            lower_flow,
            upper_flow,
            side_flow,
            lower_open,
            upper_open,
            side_open,
            settle_rate,
            gain,
        )
    sediment = sediment[:, OSTEPS : OSTEPS + row_count]
    return (sediment, waves_out)


def solution(mesh):
    return jax.shard_map(
        per_device,
        mesh=mesh,
        in_specs=(
            P("lev", ("sec", "tile"), None),
            P(("sec", "tile"), None),
            P(("sec", "tile"), None),
            P(("sec", "tile"), None),
            P(("sec", "tile"), None),
            P(("sec", "tile"), None),
            P(("sec", "tile"), None),
            P("lev"),
            P("lev"),
            P("lev"),
            P("lev", ("sec", "tile")),
            P("lev"),
            P("lev"),
            P("lev"),
            P("lev"),
            P(None, ("sec", "tile")),
            P(None, ("sec", "tile")),
            P(("sec", "tile")),
            P(("sec", "tile"), None),
            P(("sec", "tile")),
            P(("sec", "tile")),
            P(("sec", "tile"), None, None),
        ),
        out_specs=(P("lev", ("sec", "tile"), None), P("lev", ("sec", "tile"))),
        check_vma=False,
    )
```

```python
import jax
import jax.numpy as jnp
from jax import lax
from jax.experimental import pallas as pl
from jax.experimental.pallas import tpu as pltpu
from jax.sharding import PartitionSpec as P

OSTEPS = 4
WSTEPS = 4
NBRS = 4


KAPPA = 0.07
FORCE_SCALE = 5.0
DRAG = 50.0
TAU_CURRENT = 20.0
TAU_WAVES = 10.0
HIGHEST = lax.Precision.HIGHEST


def with_halo(x, sides, width):
    for axis, dim in sides:
        count, length = (lax.axis_size(axis), x.shape[dim])
        up = [(i, (i + 1) % count) for i in range(count - 1)]
        down = [(j, i) for i, j in up]
        last = lax.slice_in_dim(x, length - width, length, axis=dim)
        first = lax.slice_in_dim(x, 0, width, axis=dim)
        before = lax.ppermute(last, axis, up)
        after = lax.ppermute(first, axis, down)
        x = jnp.concatenate([before, x, after], axis=dim)
    return x


def coupling_fields(flow_lo, flow_hi, flow_y):
    eastward = 0.5 * (flow_lo.astype(jnp.float32) + flow_hi.astype(jnp.float32))
    across = flow_y.astype(jnp.float32)
    earlier = jnp.pad(across, ((0, 0), (1, 0)))[:, :-1]
    northward = 0.5 * (across + earlier)
    current_speed = jnp.sqrt(eastward * eastward + northward * northward)
    forcing = jnp.stack(
        [
            FORCE_SCALE * eastward,
            FORCE_SCALE * northward,
            DRAG * current_speed * eastward,
            DRAG * current_speed * northward,
        ]
    )
    return (forcing, eastward * eastward + northward * northward)


def band_rates(wave_forcing, band_dir, band_pace, growth, facing):
    cosines = jnp.cos(band_dir)[:, None]
    sine_terms = jnp.sin(band_dir)[:, None]
    drift_term = cosines * wave_forcing[0][None, :] + sine_terms * wave_forcing[1][None, :]
    push_term = jnp.maximum(
        cosines * wave_forcing[2][None, :] + sine_terms * wave_forcing[3][None, :], 0.0
    )
    base_rate = 0.5 * band_pace[:, None] * (1.0 + 0.5 * jnp.tanh(drift_term))
    facing_cos = jnp.cos(facing)[:, None, :]
    facing_sin = jnp.sin(facing)[:, None, :]
    along = cosines[None] * facing_cos + sine_terms[None] * facing_sin
    inflow = base_rate[None] * jnp.maximum(-along, 0.0)
    return (growth[:, None] * push_term, inflow)


def split2(x):
    hi = lax.reduce_precision(x, exponent_bits=8, mantissa_bits=7)
    return hi.astype(jnp.bfloat16), (x - hi).astype(jnp.bfloat16)


def sweep_kernel(
    left_ref, energy_ref, right_ref, sel_ref, inflow_ref, rate_ref, alive_ref, out_ref, first_ref, last_ref
):
    bands = out_ref.shape[0]
    tiles = sel_ref.shape[0]
    blocks = (
        [left_ref[...]]
        + [energy_ref[:, 128 * t : 128 * t + 128] for t in range(tiles)]
        + [right_ref[...]]
    )
    pieces = [split2(block) for block in blocks]
    for t in range(tiles):
        parts = jnp.concatenate(
            [jnp.concatenate([pieces[t + b][p] for b in range(3)], axis=1) for p in range(2)],
            axis=0,
        )
        picked = jnp.dot(parts, sel_ref[t], preferred_element_type=jnp.float32)
        gathered = picked[:bands] + picked[bands:]
        cols = slice(128 * t, 128 * t + 128)
        energy = blocks[t + 1]
        arriving = inflow_ref[0, :, cols] * gathered[:, 0:128]
        for k in range(1, NBRS):
            arriving = arriving + inflow_ref[k, :, cols] * gathered[:, 128 * k : 128 * k + 128]
        fresh = energy + arriving - rate_ref[:, cols] * energy
        out_ref[:, cols] = fresh
        if t == 0:
            first_ref[...] = fresh
        if t == tiles - 1:
            last_ref[...] = fresh


def wave_sweep(left, energy, right, sel, inflow, rate, alive):
    bands, nodes = rate.shape
    vmem = pl.BlockSpec(memory_space=pltpu.VMEM)
    flops = 2 * 2 * bands * 384 * nodes * NBRS
    moved = 4 * (2 * left.size + inflow.size + 3 * rate.size) + 2 * sel.size
    edge = jax.ShapeDtypeStruct((bands, 128), jnp.float32)
    return pl.pallas_call(
        sweep_kernel,
        out_shape=(jax.ShapeDtypeStruct((bands, nodes), jnp.float32), edge, edge),
        in_specs=[vmem] * 7,
        out_specs=(vmem, vmem, vmem),
        cost_estimate=pl.CostEstimate(flops=flops, bytes_accessed=moved, transcendentals=0),
    )(left, energy, right, sel, inflow, rate, alive)


def selection(local_index):
    nbrs, nodes = local_index.shape
    tiles = nodes // 128
    start = 128 * jnp.arange(tiles, dtype=jnp.int32)
    idx = local_index.reshape(nbrs, tiles, 128) - start[None, :, None]
    rows = jnp.arange(384, dtype=jnp.int32)
    sel = idx.transpose(1, 0, 2)[:, None, :, :] == rows[None, :, None, None]
    return sel.reshape(tiles, 384, nbrs * 128).astype(jnp.bfloat16)


def ocean_step(
    sediment,
    above_rows,
    below_rows,
    flow_lo,
    flow_hi,
    flow_y,
    open_lo,
    open_hi,
    open_y,
    settle_rate,
    erosion_gain,
):
    right_cells = jnp.pad(sediment, ((0, 0), (0, 0), (0, 1)))[:, :, 1:]
    flux_lo = (
        jnp.maximum(flow_lo, 0.0) * above_rows
        + jnp.minimum(flow_lo, 0.0) * sediment
        - KAPPA * open_lo * (sediment - above_rows)
    )
    flux_hi = (
        jnp.maximum(flow_hi, 0.0) * sediment
        + jnp.minimum(flow_hi, 0.0) * below_rows
        - KAPPA * open_hi * (below_rows - sediment)
    )
    flux_y = (
        jnp.maximum(flow_y, 0.0) * sediment
        + jnp.minimum(flow_y, 0.0) * right_cells
        - KAPPA * open_y * (right_cells - sediment)
    )
    flux_left = jnp.pad(flux_y, ((0, 0), (0, 0), (1, 0)))[:, :, :-1]
    return (
        sediment
        - (flux_hi - flux_lo)
        - (flux_y - flux_left)
        - settle_rate[:, None, None] * sediment
        + erosion_gain
    )


def entry_rank(owners, peer_count):
    onehot = (owners[:, None] == jnp.arange(peer_count, dtype=jnp.int32)[None, :]).astype(jnp.int32)
    earlier = jnp.cumsum(onehot, axis=0) - onehot
    return jnp.sum(earlier * onehot, axis=1)


def per_device(
    ocean_conc,
    flow_lo,
    flow_hi,
    flow_y,
    open_lo,
    open_hi,
    open_y,
    settle_rate,
    critical_stress,
    erosion_rate,
    wave_energy,
    band_angle,
    band_speed,
    band_growth,
    band_orbital,
    neighbors,
    facing_angle,
    live_nodes,
    remap_owner,
    remap_slot,
    remap_cell,
    remap_weight,
):
    peer_count = lax.axis_size(("sec", "tile"))
    entry_count = remap_cell.shape[0]
    capacity = min(entry_count, max(2, 2 * entry_count // peer_count))
    slot_count = peer_count * capacity
    row_count, column_count = flow_lo.shape
    ocean_count = row_count * column_count // 64
    node_count = wave_energy.shape[1]
    block_count = node_count // 64
    forcing, current_square = coupling_fields(flow_lo, flow_hi, flow_y)
    weights = remap_weight.astype(jnp.float32)
    picked = jnp.transpose(forcing.reshape(4, ocean_count, 64)[:, remap_cell, :], (1, 0, 2))
    pieces = jnp.einsum("eji,eci->ecj", weights, picked, precision=HIGHEST).reshape(
        entry_count, 256
    )
    owners = remap_owner[:, 0]
    ranking = entry_rank(owners, peer_count)
    position = owners * capacity + ranking
    tagged = jnp.concatenate([pieces, remap_slot.astype(jnp.float32)[:, None]], axis=1)
    send_rows = jnp.full((slot_count, 257), -1.0, jnp.float32).at[position].set(tagged)
    packed = send_rows.reshape(peer_count, capacity * 257)
    got = lax.all_to_all(packed, ("sec", "tile"), split_axis=0, concat_axis=0, tiled=True)
    got = got.reshape(slot_count, 257)
    got_rows = got[:, :256]
    got_ids = got[:, 256].astype(jnp.int32)
    block_index = jnp.arange(block_count, dtype=jnp.int32)
    select = (got_ids[None, :] == block_index[:, None]).astype(jnp.float32)
    wave_blocks = jnp.dot(select, got_rows, precision=HIGHEST)
    wave_forcing = jnp.transpose(wave_blocks.reshape(block_count, 4, 64), (1, 0, 2)).reshape(
        4, node_count
    )
    alive_mask = live_nodes.astype(jnp.float32)[None, :]
    source_term, inflow = band_rates(
        wave_forcing, band_angle, band_speed, band_growth, facing_angle
    )
    energy = (wave_energy.astype(jnp.float32) + source_term) * alive_mask
    first_node = lax.axis_index(("sec", "tile")) * node_count
    total_rate = jnp.sum(inflow, axis=0)
    local_index = neighbors - first_node + 128
    sel = selection(local_index)
    wave_axis = ("sec", "tile")
    up = [(i, i + 1) for i in range(lax.axis_size(wave_axis) - 1)]
    down = [(j, i) for i, j in up]
    first, last = energy[:, :128], energy[:, -128:]
    live_inflow = inflow * alive_mask[None]
    live_rate = total_rate * alive_mask
    for sweep in range(WSTEPS):
        left = lax.ppermute(last, wave_axis, up)
        right = lax.ppermute(first, wave_axis, down)
        energy, first, last = wave_sweep(left, energy, right, sel, live_inflow, live_rate, alive_mask)
    waves_out = energy.astype(jnp.bfloat16)
    coefficient = jnp.stack(
        [band_orbital * jnp.cos(band_angle), band_orbital * jnp.sin(band_angle)]
    )
    orbital = lax.psum(jnp.dot(coefficient, energy, precision=HIGHEST), "lev")
    orbital_blocks = jnp.transpose(orbital.reshape(2, block_count, 64), (1, 0, 2)).reshape(
        block_count, 128
    )
    back_rows = jnp.einsum("ws,wc->sc", select, orbital_blocks, precision=HIGHEST)
    returned = lax.all_to_all(back_rows, ("sec", "tile"), split_axis=0, concat_axis=0, tiled=True)
    mine = returned[position].reshape(entry_count, 2, 64)
    spread = jnp.einsum("eji,ecj->eci", weights, mine, precision=HIGHEST).reshape(entry_count, 128)
    ocean_select = (
        remap_cell[None, :] == jnp.arange(ocean_count, dtype=jnp.int32)[:, None]
    ).astype(jnp.float32)
    ocean_blocks = jnp.dot(ocean_select, spread, precision=HIGHEST)
    ocean_orbital = jnp.transpose(ocean_blocks.reshape(ocean_count, 2, 64), (1, 0, 2)).reshape(
        2, row_count, column_count
    )
    stress = TAU_CURRENT * current_square + TAU_WAVES * (
        ocean_orbital[0] * ocean_orbital[0] + ocean_orbital[1] * ocean_orbital[1]
    )
    erosion_gain = erosion_rate[:, None, None] * jnp.maximum(
        stress[None] / critical_stress[:, None, None] - 1.0, 0.0
    )
    classes = ocean_conc.shape[0]
    fields = jnp.concatenate(
        [
            ocean_conc,
            erosion_gain,
            jnp.stack(
                [
                    flow_lo.astype(jnp.float32),
                    flow_hi.astype(jnp.float32),
                    flow_y.astype(jnp.float32),
                    open_lo.astype(jnp.float32),
                    open_hi.astype(jnp.float32),
                    open_y.astype(jnp.float32),
                ]
            ),
        ]
    )
    wide = with_halo(fields, ((("sec", "tile"), 1),), OSTEPS)
    sediment = wide[:classes]
    gain = wide[classes : 2 * classes]
    lower_flow, upper_flow, side_flow, lower_open, upper_open, side_open = (
        wide[2 * classes + k] for k in range(6)
    )
    for sweep in range(OSTEPS):
        above_rows = jnp.pad(sediment, ((0, 0), (1, 0), (0, 0)))[:, :-1]
        below_rows = jnp.pad(sediment, ((0, 0), (0, 1), (0, 0)))[:, 1:]
        sediment = ocean_step(
            sediment,
            above_rows,
            below_rows,
            lower_flow,
            upper_flow,
            side_flow,
            lower_open,
            upper_open,
            side_open,
            settle_rate,
            gain,
        )
    sediment = sediment[:, OSTEPS : OSTEPS + row_count]
    return (sediment, waves_out)


def solution(mesh):
    return jax.shard_map(
        per_device,
        mesh=mesh,
        in_specs=(
            P("lev", ("sec", "tile"), None),
            P(("sec", "tile"), None),
            P(("sec", "tile"), None),
            P(("sec", "tile"), None),
            P(("sec", "tile"), None),
            P(("sec", "tile"), None),
            P(("sec", "tile"), None),
            P("lev"),
            P("lev"),
            P("lev"),
            P("lev", ("sec", "tile")),
            P("lev"),
            P("lev"),
            P("lev"),
            P("lev"),
            P(None, ("sec", "tile")),
            P(None, ("sec", "tile")),
            P(("sec", "tile")),
            P(("sec", "tile"), None),
            P(("sec", "tile")),
            P(("sec", "tile")),
            P(("sec", "tile"), None, None),
        ),
        out_specs=(P("lev", ("sec", "tile"), None), P("lev", ("sec", "tile"))),
        check_vma=False,
    )
```
